128 devices in a mesh: row: 8 (over y, core), col: 16 (over z, x).
Axes of the slice: x: 4, y: 4, z: 4, core: 2. Of those that a mesh axis runs over, the one named last changes fastest.
Arguments:
- fock: bfloat16 [32768, 16, 2048], P('row', 'col'), may hold values from -6 to 6
- lmo_coef: bfloat16 [32768, 1024], P(('row', 'col')), may hold values from -0.078125 to 0.078125
- three_index: bfloat16 [32768, 512], P(('row', 'col')), may hold values from -6 to 6
- rotation: bfloat16 [16, 8, 1024, 512], P('col', 'row'), may hold values from -0.1875 to 0.1875
- lmo_ids: int32 [16, 8], replicated, may hold values from 0 to 127, as said below
- domains: int32 [128, 8], replicated, may hold values from -1 to 255, as said below
Outputs:
- proj_fock: float32 [16, 8, 512, 512], P('col', 'row')
- three_rot: bfloat16 [16, 8, 512, 512], P('col', 'row')
The draws below stay inside these ranges and needn't reach their ends.
Inputs may be any that keep to these rules, and one draw needn't show every extreme that they name: `lmo_ids`: every LMO number appears exactly once; row o lists the 8 LMOs owned by column set o. `domains`: entry k of a list is -1 or a block of row panel k; entry 0 is never -1. The present blocks of one list lie in distinct column sets. For one owner o and one entry k, the blocks of the lists of lmo_ids[o, j] over all j lie in distinct column sets; for one j and one entry k, those of lmo_ids[o, j] over all o do too.
All inputs are finite; a program needn't handle non-finite values.
Results may differ from the reference program's by a relative error of at most 0.02.
Values may be sent and summed in bfloat16 or wider, within the bound.
No kernel may reach another device: no remote copies, remote signals or barrier semaphores. Data moves between devices by JAX's collectives and lax.ppermute only.
A program may use at most 192 MiB of HBM per device.

```python
import jax
import jax.numpy as jnp
from jax import lax

N = 32768
NOCC = 1024
NAUXD = 512
NROT = 512
BLK = 128
DBLK = 8
NPAN = 8
NCS = 16
FR = 256
BPD = 2
PB = 1
D = 1024
LMO_COL = 8
NLMO = 128


def domain_tables(key):
    subkeys = jax.random.split(jax.random.fold_in(key, 7), 6)
    slot_order = jax.random.permutation(subkeys[0], NLMO).astype(jnp.int32)
    shift_owner = jax.random.permutation(subkeys[1], NCS).astype(jnp.int32)
    shift_slot = jax.random.permutation(subkeys[2], NCS).astype(jnp.int32)[:LMO_COL]
    shift_entry = jax.random.permutation(subkeys[3], NCS).astype(jnp.int32)[:DBLK]
    col_set = (shift_owner[:, None, None] + shift_slot[None, :, None] + shift_entry[None, None, :]) % NCS
    panel_row = (jnp.arange(DBLK, dtype=jnp.int32) // PB)[None, None, :]
    sub_block = jax.random.randint(subkeys[4], (NCS, LMO_COL, DBLK), 0, BPD, dtype=jnp.int32)
    blocks = (panel_row * NCS + col_set) * BPD + sub_block
    present = jax.random.randint(subkeys[5], (NCS, LMO_COL, DBLK), 0, 4, dtype=jnp.int32) > 0
    present = present | (jnp.arange(DBLK, dtype=jnp.int32)[None, None, :] == 0)
    slot_doms = jnp.where(present, blocks, -1).astype(jnp.int32).reshape(NLMO, DBLK)
    domains = jnp.zeros((NLMO, DBLK), jnp.int32).at[slot_order].set(slot_doms)
    return (slot_order.reshape(NCS, LMO_COL), domains)


def draw_lmo_ids(key, part):
    return domain_tables(key)[0]


def draw_domains(key, part):
    return domain_tables(key)[1]


def shard_levels(key, dims, shards, low, largest):
    loudness = 1.0
    for dim, blocks in shards:
        steps = jax.random.uniform(jax.random.fold_in(jax.random.fold_in(key, 6), dim), (blocks,), jnp.float32, low / len(shards), largest / len(shards))
        loudness = loudness * jnp.repeat(jnp.exp(steps), dims[dim] // blocks).reshape((-1,) + (1,) * (len(dims) - 1 - dim))
    return loudness


def scatter_about(rng, shape, width, reach, cuts=(), kind=jnp.bfloat16):
    level = shard_levels(rng, shape, cuts, -0.22, 0.18) if cuts else 1.0
    array = jax.random.normal(rng, shape, jnp.float32) * width * level
    return jnp.minimum(jnp.maximum(array, -reach), reach).astype(kind)


def setup_inputs(seed: int = 0) -> dict:
    splits = jax.random.split(jax.random.key(seed), 7)
    return {
        "fock": scatter_about(splits[0], (N, NCS, N // NCS), 1.0, 6.0, ((0, 8), (1, 16))),
        "lmo_coef": scatter_about(splits[1], (N, NOCC), (6 * NOCC) ** -0.5, 0.078125, ((0, 128),)),
        "three_index": scatter_about(splits[2], (N, NAUXD), 1.0, 6.0, ((0, 128),)),
        "rotation": scatter_about(splits[3], (NCS, LMO_COL, D, NROT), D ** -0.5, 0.1875, ((0, 16), (1, 8))),
        "lmo_ids": draw_lmo_ids(jax.random.fold_in(splits[6], 71), 0),
        "domains": draw_domains(jax.random.fold_in(splits[6], 71), 0),
    }


def reference(fock, lmo_coef, three_index, rotation, lmo_ids, domains):
    coef_sets = lmo_coef.reshape(NPAN, NCS, FR, NOCC)

    def add_set(running, col_set):
        fock_cols = lax.dynamic_index_in_dim(fock, col_set, 1, keepdims=False)
        coef_rows = lax.dynamic_index_in_dim(coef_sets, col_set, 1, keepdims=False).reshape(NPAN * FR, NOCC)
        partial_value = jnp.dot(fock_cols, coef_rows, preferred_element_type=jnp.float32).astype(jnp.bfloat16)
        partial_value = lax.optimization_barrier(partial_value)
        return running + partial_value.astype(jnp.float32), None

    fock_coef, _ = lax.scan(add_set, jnp.zeros((N, NOCC), jnp.float32), jnp.arange(NCS, dtype=jnp.int32))
    occ_fock = jnp.dot(lmo_coef.T, fock_coef.astype(jnp.bfloat16), preferred_element_type=jnp.float32)
    correction = jnp.dot(lmo_coef, occ_fock.astype(jnp.bfloat16), preferred_element_type=jnp.float32)
    proj_rows = (fock_coef - 0.5 * correction).astype(jnp.bfloat16)
    all_rows = jnp.concatenate([lmo_coef, proj_rows, three_index], axis=1)
    slot_doms = jnp.take(domains, lmo_ids.reshape(-1), axis=0)
    slot_rots = rotation.reshape(NCS * LMO_COL, D, NROT)
    offsets = jnp.arange(BLK, dtype=jnp.int32)

    def finish(packed):
        slot_dom, slot_rot = packed
        present = slot_dom >= 0
        clipped = jnp.maximum(slot_dom, 0).astype(jnp.int32)
        row_index = (clipped[:, None] * BLK + offsets[None, :]).reshape(D).astype(jnp.int32)
        keep_rows = jnp.repeat(present, BLK, total_repeat_length=D)
        picked = jnp.take(all_rows, row_index, axis=0)
        picked = jnp.where(keep_rows[:, None], picked, jnp.zeros_like(picked))
        flat_dev = clipped // BPD
        col_set = jnp.repeat(flat_dev % NCS, BLK, total_repeat_length=D).astype(jnp.int32)
        col_base = (flat_dev // NCS) * FR + (clipped % BPD) * BLK
        col_pos = (jnp.repeat(col_base, BLK, total_repeat_length=D) + jnp.tile(offsets, DBLK)).astype(jnp.int32)
        fock_rows = jnp.take(fock, row_index, axis=0)
        domain_fock = fock_rows[:, col_set, col_pos]
        both_live = keep_rows[:, None] & keep_rows[None, :]
        domain_fock = jnp.where(both_live, domain_fock, jnp.zeros_like(domain_fock))
        coef_dom = picked[:, :NOCC]
        proj_dom = picked[:, NOCC:2 * NOCC]
        three_dom = picked[:, 2 * NOCC:]
        fock_half = jnp.dot(domain_fock, slot_rot, preferred_element_type=jnp.float32).astype(jnp.bfloat16)
        fock_rot = jnp.dot(slot_rot.T, fock_half, preferred_element_type=jnp.float32)
        coef_rot = jnp.dot(slot_rot.T, coef_dom, preferred_element_type=jnp.float32).astype(jnp.bfloat16)
        proj_rot = jnp.dot(slot_rot.T, proj_dom, preferred_element_type=jnp.float32).astype(jnp.bfloat16)
        result = fock_rot - jnp.dot(coef_rot, proj_rot.T, preferred_element_type=jnp.float32)
        result = result - jnp.dot(proj_rot, coef_rot.T, preferred_element_type=jnp.float32)
        three_out = jnp.dot(slot_rot.T, three_dom, preferred_element_type=jnp.float32).astype(jnp.bfloat16)
        return result, three_out

    proj_fock, three_rot = lax.map(finish, (slot_doms, slot_rots))
    return (proj_fock.reshape(NCS, LMO_COL, NROT, NROT), three_rot.reshape(NCS, LMO_COL, NROT, NAUXD))
```

```python
import jax
import jax.numpy as jnp
from jax import lax
from jax.sharding import PartitionSpec as P

BLK = 128
F32 = jnp.float32
BF16 = jnp.bfloat16


def pick(mask, table):
    return jnp.sum(jnp.where(mask, table, 0), axis=-1)


def body(fock, lmo_coef, three_index, rotation, lmo_ids, domains):
    num_sets = lax.axis_size("col")
    my_row = lax.axis_index("row")
    my_col = lax.axis_index("col")
    dev_rows = lmo_coef.shape[0]
    occ_width = lmo_coef.shape[1]
    dev_blocks = dev_rows // BLK
    dom_blocks = domains.shape[1]
    dom_width = dom_blocks * BLK
    panel_fock = fock[:, 0, :]
    panel_blocks = panel_fock.shape[0] // BLK
    col_blocks = panel_fock.shape[1] // BLK

    doms = jnp.take(domains, lmo_ids, axis=0)
    present = doms >= 0
    clipped = jnp.maximum(doms, 0)
    flat = clipped // dev_blocks
    cset = flat % num_sets
    sub = clipped % dev_blocks
    panel = flat // num_sets
    row_tile = cset * dev_blocks + sub
    col_tile = panel * dev_blocks + sub

    pres_k = lax.dynamic_index_in_dim(present, my_row, 2, keepdims=False)
    cset_k = lax.dynamic_index_in_dim(cset, my_row, 2, keepdims=False)
    sub_k = lax.dynamic_index_in_dim(sub, my_row, 2, keepdims=False)
    rtile_k = lax.dynamic_index_in_dim(row_tile, my_row, 2, keepdims=False)
    mine_k = pres_k & (cset_k == my_col)
    sub_range = jnp.arange(dev_blocks, dtype=jnp.int32)
    sel1 = jnp.any(mine_k[:, :, None] & (sub_k[:, :, None] == sub_range), axis=0).astype(BF16)

    mine2 = present & (cset == my_col)
    has2 = jnp.any(mine2, axis=0)
    rt = pick(mine2.transpose(1, 2, 0), jnp.broadcast_to(rtile_k.T[:, None, :], mine2.transpose(1, 2, 0).shape))
    ok1 = jnp.any(mine2.transpose(1, 2, 0) & pres_k.T[:, None, :], axis=-1)
    ct = pick(mine2.transpose(1, 2, 0), col_tile.transpose(1, 2, 0))
    fock_tiles = panel_fock.reshape(panel_blocks, BLK, col_blocks, BLK)
    send1_fock = fock_tiles[rt, :, ct, :]
    send1_fock = jnp.where((has2 & ok1)[:, :, None, None], send1_fock, jnp.zeros_like(send1_fock))

    in_rows = jnp.concatenate([lmo_coef, three_index], axis=1).reshape(dev_blocks, BLK, -1)
    send1_rows = jnp.einsum("js,sbw->jbw", sel1, in_rows, preferred_element_type=F32).astype(BF16)

    recv1_rows, recv1_fock = (
        lax.all_to_all(send1_rows, "row", 0, 0, tiled=True),
        lax.all_to_all(send1_fock, "row", 0, 0, tiled=True),
    )

    pres_j = lax.dynamic_index_in_dim(present, my_row, 1, keepdims=False)
    cset_j = lax.dynamic_index_in_dim(cset, my_row, 1, keepdims=False)
    sel2 = (pres_j & (cset_j == my_col)).astype(BF16)
    send2_rows = jnp.einsum("ok,kbw->obw", sel2, recv1_rows, preferred_element_type=F32).astype(BF16)
    send2_fock = jnp.einsum("ok,akbt->oabt", sel2, recv1_fock, preferred_element_type=F32).astype(BF16)
    recv2_rows, recv2_fock = (
        lax.all_to_all(send2_rows, "col", 0, 0, tiled=True),
        lax.all_to_all(send2_fock, "col", 0, 0, tiled=True),
    )

    pres_o = lax.dynamic_index_in_dim(pres_j, my_col, 0, keepdims=False)
    cset_o = lax.dynamic_index_in_dim(cset_j, my_col, 0, keepdims=False)
    set_range = jnp.arange(num_sets, dtype=jnp.int32)
    sel3 = (pres_o[:, None] & (cset_o[:, None] == set_range)).astype(BF16)
    rows_dom = jnp.einsum("ks,sbw->kbw", sel3, recv2_rows, preferred_element_type=F32).astype(BF16)
    rows_dom = rows_dom.reshape(dom_width, -1)
    domain_fock = jnp.einsum("ks,sabt->abkt", sel3, recv2_fock, preferred_element_type=F32).astype(BF16)
    domain_fock = domain_fock.reshape(dom_width, dom_width)

    gathered = lax.all_gather(lmo_coef, "row", axis=0, tiled=True)
    coef_b = lax.psum_scatter(
        jnp.dot(panel_fock, gathered, preferred_element_type=F32).astype(BF16),
        "col",
        scatter_dimension=0,
        tiled=True,
    )
    occ_term = jnp.einsum("ri,rj->ij", lmo_coef, coef_b, preferred_element_type=F32)
    occ_part = lax.psum_scatter(occ_term, ("row", "col"), scatter_dimension=0, tiled=True)
    occ_b = lax.all_gather(occ_part.astype(BF16), ("row", "col"), axis=0, tiled=True)

    fc_blocks = coef_b.reshape(dev_blocks, BLK, occ_width)
    fc1 = jnp.einsum("js,sbw->jbw", sel1, fc_blocks, preferred_element_type=F32).astype(BF16)
    fc1 = lax.all_to_all(fc1, "row", 0, 0, tiled=True)
    fc2 = jnp.einsum("ok,kbw->obw", sel2, fc1, preferred_element_type=F32).astype(BF16)
    fc2 = lax.all_to_all(fc2, "col", 0, 0, tiled=True)
    fc_dom = jnp.einsum("ks,sbw->kbw", sel3, fc2, preferred_element_type=F32).reshape(dom_width, occ_width)

    coef_dom = rows_dom[:, :occ_width]
    three_dom = rows_dom[:, occ_width:]
    correction = jnp.dot(coef_dom, occ_b, preferred_element_type=F32)
    proj_dom = (fc_dom - 0.5 * correction).astype(BF16)

    slot_rot = rotation[0, 0]
    fock_half = jnp.dot(domain_fock, slot_rot, preferred_element_type=F32).astype(BF16)
    fock_rot = jnp.einsum("xm,xn->mn", slot_rot, fock_half, preferred_element_type=F32)
    coef_rot = jnp.einsum("xm,xi->mi", slot_rot, coef_dom, preferred_element_type=F32).astype(BF16)
    proj_rot = jnp.einsum("xm,xi->mi", slot_rot, proj_dom, preferred_element_type=F32).astype(BF16)
    proj_fock = fock_rot - jnp.einsum("mi,ni->mn", coef_rot, proj_rot, preferred_element_type=F32)
    proj_fock = proj_fock - jnp.einsum("mi,ni->mn", proj_rot, coef_rot, preferred_element_type=F32)
    three_rot = jnp.einsum("xm,xu->mu", slot_rot, three_dom, preferred_element_type=F32).astype(BF16)
    return (proj_fock[None, None], three_rot[None, None])


def solution(mesh):
    placed = (
        P("row", "col", None),
        P(("row", "col"), None),
        P(("row", "col"), None),
        P("col", "row", None, None),
        P(),
        P(),
    )
    return jax.shard_map(
        body,
        mesh=mesh,
        in_specs=placed,
        out_specs=(P("col", "row", None, None), P("col", "row", None, None)),
        check_vma=False,
    )
```

```python
import jax
import jax.numpy as jnp
from jax import lax
from jax.sharding import PartitionSpec as P

BLK = 128
F32 = jnp.float32
BF16 = jnp.bfloat16


def pick(mask, table):
    return jnp.sum(jnp.where(mask, table, 0), axis=-1)


def body(fock, lmo_coef, three_index, rotation, lmo_ids, domains):
    num_sets = lax.axis_size("col")
    my_row = lax.axis_index("row")
    my_col = lax.axis_index("col")
    dev_rows = lmo_coef.shape[0]
    occ_width = lmo_coef.shape[1]
    dev_blocks = dev_rows // BLK
    dom_blocks = domains.shape[1]
    dom_width = dom_blocks * BLK
    panel_fock = fock[:, 0, :]
    panel_blocks = panel_fock.shape[0] // BLK
    col_blocks = panel_fock.shape[1] // BLK

    doms = jnp.take(domains, lmo_ids, axis=0)
    present = doms >= 0
    clipped = jnp.maximum(doms, 0)
    flat = clipped // dev_blocks
    cset = flat % num_sets
    sub = clipped % dev_blocks
    panel = flat // num_sets
    row_tile = cset * dev_blocks + sub
    col_tile = panel * dev_blocks + sub
    set_range = jnp.arange(num_sets, dtype=jnp.int32)
    sub_range = jnp.arange(dev_blocks, dtype=jnp.int32)

    pres_k = lax.dynamic_index_in_dim(present, my_row, 2, keepdims=False)
    cset_k = lax.dynamic_index_in_dim(cset, my_row, 2, keepdims=False)
    sub_k = lax.dynamic_index_in_dim(sub, my_row, 2, keepdims=False)
    rtile_k = lax.dynamic_index_in_dim(row_tile, my_row, 2, keepdims=False)
    mine_k = pres_k & (cset_k == my_col)
    sel_a = jnp.any(mine_k[:, :, None] & (sub_k[:, :, None] == sub_range), axis=1).astype(BF16)
    mine2 = present & (cset == my_col)
    ct = pick(mine2, col_tile)
    ok_tile = jnp.any(mine2, axis=2) & pres_k
    fock_tiles = panel_fock.reshape(panel_blocks, BLK, col_blocks, BLK)
    tiles_a = fock_tiles[rtile_k, :, ct, :]
    tiles_a = jnp.where(ok_tile[:, :, None, None], tiles_a, jnp.zeros_like(tiles_a))
    in_rows = jnp.concatenate([lmo_coef, three_index], axis=1).reshape(dev_blocks, BLK, -1)
    rows_a = jnp.einsum("os,sbw->obw", sel_a, in_rows, preferred_element_type=F32).astype(BF16)
    tiles_a = tiles_a.transpose(0, 2, 1, 3).reshape(num_sets, BLK, -1)
    recv_a = lax.all_to_all(jnp.concatenate([rows_a, tiles_a], axis=2), "col", 0, 0, tiled=True)

    pres_o = lax.dynamic_index_in_dim(present, my_col, 0, keepdims=False)
    cset_o = lax.dynamic_index_in_dim(cset, my_col, 0, keepdims=False)
    from_set = (pres_o[:, :, None] & (cset_o[:, :, None] == set_range)).astype(BF16)
    from_k = lax.dynamic_index_in_dim(from_set, my_row, 1, keepdims=False)
    row_width = in_rows.shape[2]
    rows_b = jnp.einsum("js,sbw->jbw", from_k, recv_a[:, :, :row_width], preferred_element_type=F32).astype(BF16)
    tiles_in = recv_a[:, :, row_width:].reshape(num_sets, BLK, dom_blocks, BLK)
    tiles_b = jnp.einsum("jks,sajb->jakb", from_set, tiles_in, preferred_element_type=F32).astype(BF16)
    tiles_b = tiles_b.reshape(dom_blocks, BLK, dom_width)
    recv_b = lax.all_to_all(jnp.concatenate([rows_b, tiles_b], axis=2), "row", 0, 0, tiled=True)
    rows_dom = recv_b[:, :, :row_width].reshape(dom_width, row_width)
    domain_fock = recv_b[:, :, row_width:].reshape(dom_width, dom_width)

    gathered = lax.all_gather(lmo_coef, "row", axis=0, tiled=True)
    coef_b = lax.psum_scatter(
        jnp.dot(panel_fock, gathered, preferred_element_type=F32).astype(BF16),
        "col",
        scatter_dimension=0,
        tiled=True,
    )
    occ_term = jnp.einsum("ri,rj->ij", lmo_coef, coef_b, preferred_element_type=F32)
    occ_b = lax.psum(occ_term, ("row", "col")).astype(BF16)

    fc_blocks = coef_b.reshape(dev_blocks, BLK, occ_width)
    fc_a = jnp.einsum("os,sbw->obw", sel_a, fc_blocks, preferred_element_type=F32).astype(BF16)
    fc_a = lax.all_to_all(fc_a, "col", 0, 0, tiled=True)
    fc_b = jnp.einsum("js,sbw->jbw", from_k, fc_a, preferred_element_type=F32).astype(BF16)
    fc_dom = lax.all_to_all(fc_b, "row", 0, 0, tiled=True).reshape(dom_width, occ_width)

    coef_dom = rows_dom[:, :occ_width]
    three_dom = rows_dom[:, occ_width:]
    correction = jnp.dot(coef_dom, occ_b, preferred_element_type=F32)
    proj_dom = (fc_dom.astype(F32) - 0.5 * correction).astype(BF16)

    slot_rot = rotation[0, 0]
    fock_half = jnp.dot(domain_fock, slot_rot, preferred_element_type=F32).astype(BF16)
    fock_rot = jnp.einsum("xm,xn->mn", slot_rot, fock_half, preferred_element_type=F32)
    coef_rot = jnp.einsum("xm,xi->mi", slot_rot, coef_dom, preferred_element_type=F32).astype(BF16)
    proj_rot = jnp.einsum("xm,xi->mi", slot_rot, proj_dom, preferred_element_type=F32).astype(BF16)
    proj_fock = fock_rot - jnp.einsum("mi,ni->mn", coef_rot, proj_rot, preferred_element_type=F32)
    proj_fock = proj_fock - jnp.einsum("mi,ni->mn", proj_rot, coef_rot, preferred_element_type=F32)
    three_rot = jnp.einsum("xm,xu->mu", slot_rot, three_dom, preferred_element_type=F32).astype(BF16)
    return (proj_fock[None, None], three_rot[None, None])


def solution(mesh):
    placed = (
        P("row", "col", None),
        P(("row", "col"), None),
        P(("row", "col"), None),
        P("col", "row", None, None),
        P(),
        P(),
    )
    return jax.shard_map(
        body,
        mesh=mesh,
        in_specs=placed,
        out_specs=(P("col", "row", None, None), P("col", "row", None, None)),
        check_vma=False,
    )
```

```python
import jax
import jax.numpy as jnp
from jax import lax
from jax.sharding import PartitionSpec as P

BLK = 128
F32 = jnp.float32
BF16 = jnp.bfloat16


def pick(mask, table):
    return jnp.sum(jnp.where(mask, table, 0), axis=-1)


def body(fock, lmo_coef, three_index, rotation, lmo_ids, domains):
    num_sets = lax.axis_size("col")
    my_row = lax.axis_index("row")
    my_col = lax.axis_index("col")
    dev_rows = lmo_coef.shape[0]
    occ_width = lmo_coef.shape[1]
    dev_blocks = dev_rows // BLK
    dom_blocks = domains.shape[1]
    dom_width = dom_blocks * BLK
    panel_fock = fock[:, 0, :]
    panel_blocks = panel_fock.shape[0] // BLK
    col_blocks = panel_fock.shape[1] // BLK

    doms = jnp.take(domains, lmo_ids, axis=0)
    present = doms >= 0
    clipped = jnp.maximum(doms, 0)
    flat = clipped // dev_blocks
    cset = flat % num_sets
    sub = clipped % dev_blocks
    panel = flat // num_sets
    row_tile = cset * dev_blocks + sub
    col_tile = panel * dev_blocks + sub
    set_range = jnp.arange(num_sets, dtype=jnp.int32)
    sub_range = jnp.arange(dev_blocks, dtype=jnp.int32)

    pres_k = lax.dynamic_index_in_dim(present, my_row, 2, keepdims=False)
    cset_k = lax.dynamic_index_in_dim(cset, my_row, 2, keepdims=False)
    sub_k = lax.dynamic_index_in_dim(sub, my_row, 2, keepdims=False)
    rtile_k = lax.dynamic_index_in_dim(row_tile, my_row, 2, keepdims=False)
    mine_k = pres_k & (cset_k == my_col)
    sel_a = jnp.any(mine_k[:, :, None] & (sub_k[:, :, None] == sub_range), axis=1).astype(BF16)
    mine2 = present & (cset == my_col)
    ct = pick(mine2, col_tile)
    ok_tile = jnp.any(mine2, axis=2) & pres_k
    fock_tiles = panel_fock.reshape(panel_blocks, BLK, col_blocks, BLK)
    tiles_a = fock_tiles[rtile_k, :, ct, :]
    tiles_a = jnp.where(ok_tile[:, :, None, None], tiles_a, jnp.zeros_like(tiles_a))
    in_rows = jnp.concatenate([lmo_coef, three_index], axis=1).reshape(dev_blocks, BLK, -1)
    rows_a = jnp.einsum("os,sbw->obw", sel_a, in_rows, preferred_element_type=F32).astype(BF16)
    tiles_a = tiles_a.transpose(0, 2, 1, 3).reshape(num_sets, BLK, -1)
    recv_a = lax.all_to_all(jnp.concatenate([rows_a, tiles_a], axis=2), "col", 0, 0, tiled=True)

    pres_o = lax.dynamic_index_in_dim(present, my_col, 0, keepdims=False)
    cset_o = lax.dynamic_index_in_dim(cset, my_col, 0, keepdims=False)
    from_set = (pres_o[:, :, None] & (cset_o[:, :, None] == set_range)).astype(BF16)
    from_k = lax.dynamic_index_in_dim(from_set, my_row, 1, keepdims=False)
    row_width = in_rows.shape[2]
    rows_b = jnp.einsum("js,sbw->jbw", from_k, recv_a[:, :, :row_width], preferred_element_type=F32).astype(BF16)
    tiles_in = recv_a[:, :, row_width:].reshape(num_sets, BLK, dom_blocks, BLK)
    tiles_b = jnp.einsum("jks,sajb->jakb", from_set, tiles_in, preferred_element_type=F32).astype(BF16)
    tiles_b = tiles_b.reshape(dom_blocks, BLK, dom_width)

    gathered = lax.all_gather(lmo_coef, "row", axis=0, tiled=True)
    rows_b, tiles_b, gathered = lax.optimization_barrier((rows_b, tiles_b, gathered))
    coef_b = lax.psum_scatter(
        jnp.dot(panel_fock, gathered, preferred_element_type=F32).astype(BF16),
        "col",
        scatter_dimension=0,
        tiled=True,
    )
    occ_term = jnp.einsum("ri,rj->ij", lmo_coef, coef_b, preferred_element_type=F32)
    occ_b = lax.psum(occ_term, ("row", "col")).astype(BF16)

    fc_blocks = coef_b.reshape(dev_blocks, BLK, occ_width)
    fc_a = jnp.einsum("os,sbw->obw", sel_a, fc_blocks, preferred_element_type=F32).astype(BF16)
    fc_a = lax.all_to_all(fc_a, "col", 0, 0, tiled=True)
    fc_b = jnp.einsum("js,sbw->jbw", from_k, fc_a, preferred_element_type=F32).astype(BF16)
    recv_b = lax.all_to_all(jnp.concatenate([rows_b, tiles_b, fc_b], axis=2), "row", 0, 0, tiled=True)
    rows_dom = recv_b[:, :, :row_width].reshape(dom_width, row_width)
    domain_fock = recv_b[:, :, row_width : row_width + dom_width].reshape(dom_width, dom_width)
    fc_dom = recv_b[:, :, row_width + dom_width :].reshape(dom_width, occ_width)

    coef_dom = rows_dom[:, :occ_width]
    three_dom = rows_dom[:, occ_width:]
    correction = jnp.dot(coef_dom, occ_b, preferred_element_type=F32)
    proj_dom = (fc_dom.astype(F32) - 0.5 * correction).astype(BF16)

    slot_rot = rotation[0, 0]
    fock_half = jnp.dot(domain_fock, slot_rot, preferred_element_type=F32).astype(BF16)
    fock_rot = jnp.einsum("xm,xn->mn", slot_rot, fock_half, preferred_element_type=F32)
    coef_rot = jnp.einsum("xm,xi->mi", slot_rot, coef_dom, preferred_element_type=F32).astype(BF16)
    proj_rot = jnp.einsum("xm,xi->mi", slot_rot, proj_dom, preferred_element_type=F32).astype(BF16)
    proj_fock = fock_rot - jnp.einsum("mi,ni->mn", coef_rot, proj_rot, preferred_element_type=F32)
    proj_fock = proj_fock - jnp.einsum("mi,ni->mn", proj_rot, coef_rot, preferred_element_type=F32)
    three_rot = jnp.einsum("xm,xu->mu", slot_rot, three_dom, preferred_element_type=F32).astype(BF16)
    return (proj_fock[None, None], three_rot[None, None])


def solution(mesh):
    placed = (
        P("row", "col", None),
        P(("row", "col"), None),
        P(("row", "col"), None),
        P("col", "row", None, None),
        P(),
        P(),
    )
    return jax.shard_map(
        body,
        mesh=mesh,
        in_specs=placed,
        out_specs=(P("col", "row", None, None), P("col", "row", None, None)),
        check_vma=False,
    )
```

```python
import jax
import jax.numpy as jnp
from jax import lax
from jax.sharding import PartitionSpec as P

BLK = 128
F32 = jnp.float32
BF16 = jnp.bfloat16


def pick(mask, table):
    return jnp.sum(jnp.where(mask, table, 0), axis=-1)


def body(fock, lmo_coef, three_index, rotation, lmo_ids, domains):
    num_sets = lax.axis_size("col")
    my_row = lax.axis_index("row")
    my_col = lax.axis_index("col")
    dev_rows = lmo_coef.shape[0]
    occ_width = lmo_coef.shape[1]
    dev_blocks = dev_rows // BLK
    dom_blocks = domains.shape[1]
    dom_width = dom_blocks * BLK
    panel_fock = fock[:, 0, :]
    panel_blocks = panel_fock.shape[0] // BLK
    col_blocks = panel_fock.shape[1] // BLK

    doms = jnp.take(domains, lmo_ids, axis=0)
    present = doms >= 0
    clipped = jnp.maximum(doms, 0)
    flat = clipped // dev_blocks
    cset = flat % num_sets
    sub = clipped % dev_blocks
    panel = flat // num_sets
    row_tile = cset * dev_blocks + sub
    col_tile = panel * dev_blocks + sub
    set_range = jnp.arange(num_sets, dtype=jnp.int32)
    sub_range = jnp.arange(dev_blocks, dtype=jnp.int32)

    pres_k = lax.dynamic_index_in_dim(present, my_row, 2, keepdims=False)
    cset_k = lax.dynamic_index_in_dim(cset, my_row, 2, keepdims=False)
    sub_k = lax.dynamic_index_in_dim(sub, my_row, 2, keepdims=False)
    rtile_k = lax.dynamic_index_in_dim(row_tile, my_row, 2, keepdims=False)
    mine_k = pres_k & (cset_k == my_col)
    has_o = jnp.any(mine_k, axis=1)
    sub_o = pick(mine_k, sub_k)
    mine2 = present & (cset == my_col)
    ct = pick(mine2, col_tile)
    ok_tile = jnp.any(mine2, axis=2) & pres_k
    fock_tiles = panel_fock.reshape(panel_blocks, BLK, col_blocks, BLK)
    tiles_a = fock_tiles[rtile_k, :, ct, :]
    tiles_a = jnp.where(ok_tile[:, :, None, None], tiles_a, jnp.zeros_like(tiles_a))
    in_rows = jnp.concatenate([lmo_coef, three_index], axis=1).reshape(dev_blocks, BLK, -1)
    rows_a = jnp.take(in_rows, sub_o, axis=0)
    rows_a = jnp.where(has_o[:, None, None], rows_a, jnp.zeros_like(rows_a))
    rows_a, tiles_a = (
        lax.all_to_all(rows_a, "col", 0, 0, tiled=True),
        lax.all_to_all(tiles_a, "col", 0, 0, tiled=True),
    )

    pres_o = lax.dynamic_index_in_dim(present, my_col, 0, keepdims=False)
    cset_o = lax.dynamic_index_in_dim(cset, my_col, 0, keepdims=False)
    pres_jk = lax.dynamic_index_in_dim(pres_o, my_row, 1, keepdims=False)
    cset_jk = lax.dynamic_index_in_dim(cset_o, my_row, 1, keepdims=False)
    rows_b = jnp.take(rows_a, cset_jk, axis=0)
    rows_b = jnp.where(pres_jk[:, None, None], rows_b, jnp.zeros_like(rows_b))
    slot_ids = jnp.broadcast_to(jnp.arange(dom_blocks, dtype=jnp.int32)[:, None], cset_o.shape)
    tiles_b = tiles_a[cset_o, slot_ids]
    tiles_b = jnp.where(pres_o[:, :, None, None], tiles_b, jnp.zeros_like(tiles_b))
    rows_dom, tiles_dom = (
        lax.all_to_all(rows_b, "row", 0, 0, tiled=True),
        lax.all_to_all(tiles_b, "row", 0, 0, tiled=True),
    )
    rows_dom = rows_dom.reshape(dom_width, -1)

    gathered = lax.all_gather(lmo_coef, "row", axis=0, tiled=True)
    coef_b = lax.psum_scatter(
        jnp.dot(panel_fock, gathered, preferred_element_type=F32).astype(BF16),
        "col",
        scatter_dimension=0,
        tiled=True,
    )
    occ_term = jnp.einsum("ri,rj->ij", lmo_coef, coef_b, preferred_element_type=F32)
    occ_b = lax.psum(occ_term, ("row", "col")).astype(BF16)

    fc_a = jnp.take(coef_b.reshape(dev_blocks, BLK, occ_width), sub_o, axis=0)
    fc_a = jnp.where(has_o[:, None, None], fc_a, jnp.zeros_like(fc_a))
    fc_a = lax.all_to_all(fc_a, "col", 0, 0, tiled=True)
    fc_b = jnp.take(fc_a, cset_jk, axis=0)
    fc_b = jnp.where(pres_jk[:, None, None], fc_b, jnp.zeros_like(fc_b))
    fc_dom = lax.all_to_all(fc_b, "row", 0, 0, tiled=True).reshape(dom_width, occ_width)

    coef_dom = rows_dom[:, :occ_width]
    three_dom = rows_dom[:, occ_width:]
    correction = jnp.dot(coef_dom, occ_b, preferred_element_type=F32)
    proj_dom = (fc_dom.astype(F32) - 0.5 * correction).astype(BF16)

    slot_rot = rotation[0, 0]
    rot_tiles = slot_rot.reshape(dom_blocks, BLK, -1)
    fock_half = jnp.einsum("abtu,bun->atn", tiles_dom, rot_tiles, preferred_element_type=F32)
    fock_half = fock_half.reshape(dom_width, -1).astype(BF16)
    fock_rot = jnp.einsum("xm,xn->mn", slot_rot, fock_half, preferred_element_type=F32)
    coef_rot = jnp.einsum("xm,xi->mi", slot_rot, coef_dom, preferred_element_type=F32).astype(BF16)
    proj_rot = jnp.einsum("xm,xi->mi", slot_rot, proj_dom, preferred_element_type=F32).astype(BF16)
    proj_fock = fock_rot - jnp.einsum("mi,ni->mn", coef_rot, proj_rot, preferred_element_type=F32)
    proj_fock = proj_fock - jnp.einsum("mi,ni->mn", proj_rot, coef_rot, preferred_element_type=F32)
    three_rot = jnp.einsum("xm,xu->mu", slot_rot, three_dom, preferred_element_type=F32).astype(BF16)
    return (proj_fock[None, None], three_rot[None, None])


def solution(mesh):
    placed = (
        P("row", "col", None),
        P(("row", "col"), None),
        P(("row", "col"), None),
        P("col", "row", None, None),
        P(),
        P(),
    )
    return jax.shard_map(
        body,
        mesh=mesh,
        in_specs=placed,
        out_specs=(P("col", "row", None, None), P("col", "row", None, None)),
        check_vma=False,
    )
```

```python
import jax
import jax.numpy as jnp
from jax import lax
from jax.sharding import PartitionSpec as P

BLK = 128
F32 = jnp.float32
BF16 = jnp.bfloat16


def pick(mask, table):
    return jnp.sum(jnp.where(mask, table, 0), axis=-1)


def body(fock, lmo_coef, three_index, rotation, lmo_ids, domains):
    num_sets = lax.axis_size("col")
    my_row = lax.axis_index("row")
    my_col = lax.axis_index("col")
    dev_rows = lmo_coef.shape[0]
    occ_width = lmo_coef.shape[1]
    dev_blocks = dev_rows // BLK
    dom_blocks = domains.shape[1]
    dom_width = dom_blocks * BLK
    panel_fock = fock[:, 0, :]
    panel_blocks = panel_fock.shape[0] // BLK
    col_blocks = panel_fock.shape[1] // BLK

    doms = jnp.take(domains, lmo_ids, axis=0)
    present = doms >= 0
    clipped = jnp.maximum(doms, 0)
    flat = clipped // dev_blocks
    cset = flat % num_sets
    sub = clipped % dev_blocks
    panel = flat // num_sets
    row_tile = cset * dev_blocks + sub
    col_tile = panel * dev_blocks + sub

    pres_k = lax.dynamic_index_in_dim(present, my_row, 2, keepdims=False)
    cset_k = lax.dynamic_index_in_dim(cset, my_row, 2, keepdims=False)
    sub_k = lax.dynamic_index_in_dim(sub, my_row, 2, keepdims=False)
    rtile_k = lax.dynamic_index_in_dim(row_tile, my_row, 2, keepdims=False)
    mine_k = pres_k & (cset_k == my_col)
    has_o = jnp.any(mine_k, axis=1)
    sub_o = pick(mine_k, sub_k)
    mine2 = present & (cset == my_col)
    ct = pick(mine2, col_tile)
    ok_tile = jnp.any(mine2, axis=2) & pres_k
    fock_tiles = panel_fock.reshape(panel_blocks, BLK, col_blocks, BLK)
    tiles_a = fock_tiles[rtile_k, :, ct, :]
    tiles_a = jnp.where(ok_tile[:, :, None, None], tiles_a, jnp.zeros_like(tiles_a))
    in_rows = jnp.concatenate([lmo_coef, three_index], axis=1).reshape(dev_blocks, BLK, -1)
    rows_a = jnp.take(in_rows, sub_o, axis=0)
    rows_a = jnp.where(has_o[:, None, None], rows_a, jnp.zeros_like(rows_a))
    rows_a, tiles_a = (
        lax.all_to_all(rows_a, "col", 0, 0, tiled=True),
        lax.all_to_all(tiles_a, "col", 0, 0, tiled=True),
    )

    gathered = lax.all_gather(lmo_coef, "row", axis=0, tiled=True)
    coef_b = lax.psum_scatter(
        jnp.dot(panel_fock, gathered, preferred_element_type=F32).astype(BF16),
        "col",
        scatter_dimension=0,
        tiled=True,
    )
    occ_term = jnp.einsum("ri,rj->ij", lmo_coef, coef_b, preferred_element_type=F32)
    occ_b = lax.psum(occ_term, ("row", "col")).astype(BF16)

    fc_a = jnp.take(coef_b.reshape(dev_blocks, BLK, occ_width), sub_o, axis=0)
    fc_a = jnp.where(has_o[:, None, None], fc_a, jnp.zeros_like(fc_a))
    fc_a = lax.all_to_all(fc_a, "col", 0, 0, tiled=True)

    pres_o = lax.dynamic_index_in_dim(present, my_col, 0, keepdims=False)
    cset_o = lax.dynamic_index_in_dim(cset, my_col, 0, keepdims=False)
    pres_jk = lax.dynamic_index_in_dim(pres_o, my_row, 1, keepdims=False)
    cset_jk = lax.dynamic_index_in_dim(cset_o, my_row, 1, keepdims=False)
    rows_a, tiles_a, fc_a, occ_b = lax.optimization_barrier((rows_a, tiles_a, fc_a, occ_b))
    rows_b = jnp.take(rows_a, cset_jk, axis=0)
    rows_b = jnp.where(pres_jk[:, None, None], rows_b, jnp.zeros_like(rows_b))
    slot_ids = jnp.broadcast_to(jnp.arange(dom_blocks, dtype=jnp.int32)[:, None], cset_o.shape)
    tiles_b = tiles_a[cset_o, slot_ids]
    tiles_b = jnp.where(pres_o[:, :, None, None], tiles_b, jnp.zeros_like(tiles_b))
    rows_dom, tiles_dom = (
        lax.all_to_all(rows_b, "row", 0, 0, tiled=True),
        lax.all_to_all(tiles_b, "row", 0, 0, tiled=True),
    )
    rows_dom = rows_dom.reshape(dom_width, -1)

    fc_b = jnp.take(fc_a, cset_jk, axis=0)
    fc_b = jnp.where(pres_jk[:, None, None], fc_b, jnp.zeros_like(fc_b))
    fc_dom = lax.all_to_all(fc_b, "row", 0, 0, tiled=True).reshape(dom_width, occ_width)

    coef_dom = rows_dom[:, :occ_width]
    three_dom = rows_dom[:, occ_width:]
    correction = jnp.dot(coef_dom, occ_b, preferred_element_type=F32)
    proj_dom = (fc_dom.astype(F32) - 0.5 * correction).astype(BF16)

    slot_rot = rotation[0, 0]
    rot_tiles = slot_rot.reshape(dom_blocks, BLK, -1)
    fock_half = jnp.einsum("abtu,bun->atn", tiles_dom, rot_tiles, preferred_element_type=F32)
    fock_half = fock_half.reshape(dom_width, -1).astype(BF16)
    fock_rot = jnp.einsum("xm,xn->mn", slot_rot, fock_half, preferred_element_type=F32)
    coef_rot = jnp.einsum("xm,xi->mi", slot_rot, coef_dom, preferred_element_type=F32).astype(BF16)
    proj_rot = jnp.einsum("xm,xi->mi", slot_rot, proj_dom, preferred_element_type=F32).astype(BF16)
    proj_fock = fock_rot - jnp.einsum("mi,ni->mn", coef_rot, proj_rot, preferred_element_type=F32)
    proj_fock = proj_fock - jnp.einsum("mi,ni->mn", proj_rot, coef_rot, preferred_element_type=F32)
    three_rot = jnp.einsum("xm,xu->mu", slot_rot, three_dom, preferred_element_type=F32).astype(BF16)
    return (proj_fock[None, None], three_rot[None, None])


def solution(mesh):
    placed = (
        P("row", "col", None),
        P(("row", "col"), None),
        P(("row", "col"), None),
        P("col", "row", None, None),
        P(),
        P(),
    )
    return jax.shard_map(
        body,
        mesh=mesh,
        in_specs=placed,
        out_specs=(P("col", "row", None, None), P("col", "row", None, None)),
        check_vma=False,
    )
```

```python
import jax
import jax.numpy as jnp
from jax import lax
from jax.sharding import PartitionSpec as P

BLK = 128
F32 = jnp.float32
BF16 = jnp.bfloat16


def pick(mask, table):
    return jnp.sum(jnp.where(mask, table, 0), axis=-1)


def body(fock, lmo_coef, three_index, rotation, lmo_ids, domains):
    num_sets = lax.axis_size("col")
    my_row = lax.axis_index("row")
    my_col = lax.axis_index("col")
    dev_rows = lmo_coef.shape[0]
    occ_width = lmo_coef.shape[1]
    dev_blocks = dev_rows // BLK
    dom_blocks = domains.shape[1]
    dom_width = dom_blocks * BLK
    panel_fock = fock[:, 0, :]
    panel_blocks = panel_fock.shape[0] // BLK
    col_blocks = panel_fock.shape[1] // BLK

    doms = jnp.take(domains, lmo_ids, axis=0)
    present = doms >= 0
    clipped = jnp.maximum(doms, 0)
    flat = clipped // dev_blocks
    cset = flat % num_sets
    sub = clipped % dev_blocks
    panel = flat // num_sets
    row_tile = cset * dev_blocks + sub
    col_tile = panel * dev_blocks + sub

    pres_k = lax.dynamic_index_in_dim(present, my_row, 2, keepdims=False)
    cset_k = lax.dynamic_index_in_dim(cset, my_row, 2, keepdims=False)
    sub_k = lax.dynamic_index_in_dim(sub, my_row, 2, keepdims=False)
    rtile_k = lax.dynamic_index_in_dim(row_tile, my_row, 2, keepdims=False)
    mine_k = pres_k & (cset_k == my_col)
    has_o = jnp.any(mine_k, axis=1)
    sub_o = pick(mine_k, sub_k)
    mine2 = present & (cset == my_col)
    ct = pick(mine2, col_tile)
    ok_tile = jnp.any(mine2, axis=2) & pres_k
    fock_tiles = panel_fock.reshape(panel_blocks, BLK, col_blocks, BLK)
    tiles_a = fock_tiles[rtile_k, :, ct, :]
    tiles_a = jnp.where(ok_tile[:, :, None, None], tiles_a, jnp.zeros_like(tiles_a))
    in_rows = jnp.concatenate([lmo_coef, three_index], axis=1).reshape(dev_blocks, BLK, -1)
    rows_a = jnp.take(in_rows, sub_o, axis=0)
    rows_a = jnp.where(has_o[:, None, None], rows_a, jnp.zeros_like(rows_a))
    rows_a = lax.all_to_all(rows_a, "col", 0, 0, tiled=True)
    tiles_a = lax.all_to_all(tiles_a, "col", 0, 0, tiled=True)

    gathered = lax.all_gather(lmo_coef, "row", axis=0, tiled=True)
    fock_lmo = jnp.dot(panel_fock, gathered, preferred_element_type=F32).astype(BF16)
    rows_a, fock_lmo = lax.optimization_barrier((rows_a, fock_lmo))
    coef_b = lax.psum_scatter(
        fock_lmo,
        "col",
        scatter_dimension=0,
        tiled=True,
    )
    occ_term = jnp.einsum("ri,rj->ij", lmo_coef, coef_b, preferred_element_type=F32)
    occ_b = lax.psum(occ_term, ("row", "col")).astype(BF16)

    pres_o = lax.dynamic_index_in_dim(present, my_col, 0, keepdims=False)
    cset_o = lax.dynamic_index_in_dim(cset, my_col, 0, keepdims=False)
    pres_jk = lax.dynamic_index_in_dim(pres_o, my_row, 1, keepdims=False)
    cset_jk = lax.dynamic_index_in_dim(cset_o, my_row, 1, keepdims=False)
    rows_b = jnp.take(rows_a, cset_jk, axis=0)
    rows_b = jnp.where(pres_jk[:, None, None], rows_b, jnp.zeros_like(rows_b))
    slot_ids = jnp.broadcast_to(jnp.arange(dom_blocks, dtype=jnp.int32)[:, None], cset_o.shape)
    tiles_b = tiles_a[cset_o, slot_ids]
    tiles_b = jnp.where(pres_o[:, :, None, None], tiles_b, jnp.zeros_like(tiles_b))
    rows_dom, tiles_dom = (
        lax.all_to_all(rows_b, "row", 0, 0, tiled=True),
        lax.all_to_all(tiles_b, "row", 0, 0, tiled=True),
    )
    rows_dom = rows_dom.reshape(dom_width, -1)

    fc_a = jnp.take(coef_b.reshape(dev_blocks, BLK, occ_width), sub_o, axis=0)
    fc_a = jnp.where(has_o[:, None, None], fc_a, jnp.zeros_like(fc_a))
    fc_a = lax.all_to_all(fc_a, "col", 0, 0, tiled=True)
    fc_b = jnp.take(fc_a, cset_jk, axis=0)
    fc_b = jnp.where(pres_jk[:, None, None], fc_b, jnp.zeros_like(fc_b))
    fc_dom = lax.all_to_all(fc_b, "row", 0, 0, tiled=True).reshape(dom_width, occ_width)

    coef_dom = rows_dom[:, :occ_width]
    three_dom = rows_dom[:, occ_width:]
    correction = jnp.dot(coef_dom, occ_b, preferred_element_type=F32)
    proj_dom = (fc_dom.astype(F32) - 0.5 * correction).astype(BF16)

    slot_rot = rotation[0, 0]
    rot_tiles = slot_rot.reshape(dom_blocks, BLK, -1)
    fock_half = jnp.einsum("abtu,bun->atn", tiles_dom, rot_tiles, preferred_element_type=F32)
    fock_half = fock_half.reshape(dom_width, -1).astype(BF16)
    fock_rot = jnp.einsum("xm,xn->mn", slot_rot, fock_half, preferred_element_type=F32)
    coef_rot = jnp.einsum("xm,xi->mi", slot_rot, coef_dom, preferred_element_type=F32).astype(BF16)
    proj_rot = jnp.einsum("xm,xi->mi", slot_rot, proj_dom, preferred_element_type=F32).astype(BF16)
    proj_fock = fock_rot - jnp.einsum("mi,ni->mn", coef_rot, proj_rot, preferred_element_type=F32)
    proj_fock = proj_fock - jnp.einsum("mi,ni->mn", proj_rot, coef_rot, preferred_element_type=F32)
    three_rot = jnp.einsum("xm,xu->mu", slot_rot, three_dom, preferred_element_type=F32).astype(BF16)
    return (proj_fock[None, None], three_rot[None, None])


def solution(mesh):
    placed = (
        P("row", "col", None),
        P(("row", "col"), None),
        P(("row", "col"), None),
        P("col", "row", None, None),
        P(),
        P(),
    )
    return jax.shard_map(
        body,
        mesh=mesh,
        in_specs=placed,
        out_specs=(P("col", "row", None, None), P("col", "row", None, None)),
        check_vma=False,
    )
```

```python
import jax
import jax.numpy as jnp
from jax import lax
from jax.sharding import PartitionSpec as P

BLK = 128
F32 = jnp.float32
BF16 = jnp.bfloat16


def pick(mask, table):
    return jnp.sum(jnp.where(mask, table, 0), axis=-1)


def body(fock, lmo_coef, three_index, rotation, lmo_ids, domains):
    num_sets = lax.axis_size("col")
    my_row = lax.axis_index("row")
    my_col = lax.axis_index("col")
    dev_rows = lmo_coef.shape[0]
    occ_width = lmo_coef.shape[1]
    dev_blocks = dev_rows // BLK
    dom_blocks = domains.shape[1]
    dom_width = dom_blocks * BLK
    panel_fock = fock[:, 0, :]
    panel_blocks = panel_fock.shape[0] // BLK
    col_blocks = panel_fock.shape[1] // BLK

    doms = jnp.take(domains, lmo_ids, axis=0)
    present = doms >= 0
    clipped = jnp.maximum(doms, 0)
    flat = clipped // dev_blocks
    cset = flat % num_sets
    sub = clipped % dev_blocks
    panel = flat // num_sets
    row_tile = cset * dev_blocks + sub
    col_tile = panel * dev_blocks + sub

    pres_k = lax.dynamic_index_in_dim(present, my_row, 2, keepdims=False)
    cset_k = lax.dynamic_index_in_dim(cset, my_row, 2, keepdims=False)
    sub_k = lax.dynamic_index_in_dim(sub, my_row, 2, keepdims=False)
    rtile_k = lax.dynamic_index_in_dim(row_tile, my_row, 2, keepdims=False)
    mine_k = pres_k & (cset_k == my_col)
    has_o = jnp.any(mine_k, axis=1)
    sub_o = pick(mine_k, sub_k)
    mine2 = present & (cset == my_col)
    ct = pick(mine2, col_tile)
    ok_tile = jnp.any(mine2, axis=2) & pres_k
    fock_tiles = panel_fock.reshape(panel_blocks, BLK, col_blocks, BLK)
    tiles_a = fock_tiles[rtile_k, :, ct, :]
    tiles_a = jnp.where(ok_tile[:, :, None, None], tiles_a, jnp.zeros_like(tiles_a))
    in_rows = jnp.concatenate([lmo_coef, three_index], axis=1).reshape(dev_blocks, BLK, -1)
    rows_a = jnp.take(in_rows, sub_o, axis=0)
    rows_a = jnp.where(has_o[:, None, None], rows_a, jnp.zeros_like(rows_a))
    rows_a = lax.all_to_all(rows_a, "col", 0, 0, tiled=True)
    tiles_a = lax.all_to_all(tiles_a, "col", 0, 0, tiled=True)

    gathered = lax.all_gather(lmo_coef, "row", axis=0, tiled=True)
    fock_lmo = jnp.dot(panel_fock, gathered, preferred_element_type=F32).astype(BF16)
    rows_a, tiles_a, fock_lmo = lax.optimization_barrier((rows_a, tiles_a, fock_lmo))
    coef_b = lax.psum_scatter(
        fock_lmo,
        "col",
        scatter_dimension=0,
        tiled=True,
    )
    occ_term = jnp.einsum("ri,rj->ij", lmo_coef, coef_b, preferred_element_type=F32)
    occ_b = lax.psum(occ_term, ("row", "col")).astype(BF16)

    pres_o = lax.dynamic_index_in_dim(present, my_col, 0, keepdims=False)
    cset_o = lax.dynamic_index_in_dim(cset, my_col, 0, keepdims=False)
    pres_jk = lax.dynamic_index_in_dim(pres_o, my_row, 1, keepdims=False)
    cset_jk = lax.dynamic_index_in_dim(cset_o, my_row, 1, keepdims=False)
    rows_b = jnp.take(rows_a, cset_jk, axis=0)
    rows_b = jnp.where(pres_jk[:, None, None], rows_b, jnp.zeros_like(rows_b))
    slot_ids = jnp.broadcast_to(jnp.arange(dom_blocks, dtype=jnp.int32)[:, None], cset_o.shape)
    tiles_b = tiles_a[cset_o, slot_ids]
    tiles_b = jnp.where(pres_o[:, :, None, None], tiles_b, jnp.zeros_like(tiles_b))
    rows_dom, tiles_dom = (
        lax.all_to_all(rows_b, "row", 0, 0, tiled=True),
        lax.all_to_all(tiles_b, "row", 0, 0, tiled=True),
    )
    rows_dom = rows_dom.reshape(dom_width, -1)

    fc_a = jnp.take(coef_b.reshape(dev_blocks, BLK, occ_width), sub_o, axis=0)
    fc_a = jnp.where(has_o[:, None, None], fc_a, jnp.zeros_like(fc_a))
    fc_a = lax.all_to_all(fc_a, "col", 0, 0, tiled=True)
    fc_b = jnp.take(fc_a, cset_jk, axis=0)
    fc_b = jnp.where(pres_jk[:, None, None], fc_b, jnp.zeros_like(fc_b))
    fc_dom = lax.all_to_all(fc_b, "row", 0, 0, tiled=True).reshape(dom_width, occ_width)

    coef_dom = rows_dom[:, :occ_width]
    three_dom = rows_dom[:, occ_width:]
    correction = jnp.dot(coef_dom, occ_b, preferred_element_type=F32)
    proj_dom = (fc_dom.astype(F32) - 0.5 * correction).astype(BF16)

    slot_rot = rotation[0, 0]
    rot_tiles = slot_rot.reshape(dom_blocks, BLK, -1)
    fock_half = jnp.einsum("abtu,bun->atn", tiles_dom, rot_tiles, preferred_element_type=F32)
    fock_half = fock_half.reshape(dom_width, -1).astype(BF16)
    fock_rot = jnp.einsum("xm,xn->mn", slot_rot, fock_half, preferred_element_type=F32)
    coef_rot = jnp.einsum("xm,xi->mi", slot_rot, coef_dom, preferred_element_type=F32).astype(BF16)
    proj_rot = jnp.einsum("xm,xi->mi", slot_rot, proj_dom, preferred_element_type=F32).astype(BF16)
    proj_fock = fock_rot - jnp.einsum("mi,ni->mn", coef_rot, proj_rot, preferred_element_type=F32)
    proj_fock = proj_fock - jnp.einsum("mi,ni->mn", proj_rot, coef_rot, preferred_element_type=F32)
    three_rot = jnp.einsum("xm,xu->mu", slot_rot, three_dom, preferred_element_type=F32).astype(BF16)
    return (proj_fock[None, None], three_rot[None, None])


def solution(mesh):
    placed = (
        P("row", "col", None),
        P(("row", "col"), None),
        P(("row", "col"), None),
        P("col", "row", None, None),
        P(),
        P(),
    )
    return jax.shard_map(
        body,
        mesh=mesh,
        in_specs=placed,
        out_specs=(P("col", "row", None, None), P("col", "row", None, None)),
        check_vma=False,
    )
```

```python
import jax
import jax.numpy as jnp
from jax import lax
from jax.sharding import PartitionSpec as P

BLK = 128
F32 = jnp.float32
BF16 = jnp.bfloat16


def pick(mask, table):
    return jnp.sum(jnp.where(mask, table, 0), axis=-1)


def body(fock, lmo_coef, three_index, rotation, lmo_ids, domains):
    num_sets = lax.axis_size("col")
    my_row = lax.axis_index("row")
    my_col = lax.axis_index("col")
    dev_rows = lmo_coef.shape[0]
    occ_width = lmo_coef.shape[1]
    dev_blocks = dev_rows // BLK
    dom_blocks = domains.shape[1]
    dom_width = dom_blocks * BLK
    panel_fock = fock[:, 0, :]
    panel_blocks = panel_fock.shape[0] // BLK
    col_blocks = panel_fock.shape[1] // BLK

    doms = jnp.take(domains, lmo_ids, axis=0)
    present = doms >= 0
    clipped = jnp.maximum(doms, 0)
    flat = clipped // dev_blocks
    cset = flat % num_sets
    sub = clipped % dev_blocks
    panel = flat // num_sets
    row_tile = cset * dev_blocks + sub
    col_tile = panel * dev_blocks + sub

    pres_k = lax.dynamic_index_in_dim(present, my_row, 2, keepdims=False)
    cset_k = lax.dynamic_index_in_dim(cset, my_row, 2, keepdims=False)
    sub_k = lax.dynamic_index_in_dim(sub, my_row, 2, keepdims=False)
    rtile_k = lax.dynamic_index_in_dim(row_tile, my_row, 2, keepdims=False)
    mine_k = pres_k & (cset_k == my_col)
    has_o = jnp.any(mine_k, axis=1)
    sub_o = pick(mine_k, sub_k)
    mine2 = present & (cset == my_col)
    ct = pick(mine2, col_tile)
    ok_tile = jnp.any(mine2, axis=2) & pres_k
    fock_tiles = panel_fock.reshape(panel_blocks, BLK, col_blocks, BLK)
    tiles_a = fock_tiles[rtile_k, :, ct, :]
    tiles_a = jnp.where(ok_tile[:, :, None, None], tiles_a, jnp.zeros_like(tiles_a))
    in_rows = jnp.concatenate([lmo_coef, three_index], axis=1).reshape(dev_blocks, BLK, -1)
    rows_a = jnp.take(in_rows, sub_o, axis=0)
    rows_a = jnp.where(has_o[:, None, None], rows_a, jnp.zeros_like(rows_a))
    rows_a = lax.all_to_all(rows_a, "col", 0, 0, tiled=True)
    tiles_a, rows_a = lax.optimization_barrier((tiles_a, rows_a))
    tiles_a = lax.all_to_all(tiles_a, "col", 0, 0, tiled=True)

    gathered = lax.all_gather(lmo_coef, "row", axis=0, tiled=True)
    fock_lmo = jnp.dot(panel_fock, gathered, preferred_element_type=F32).astype(BF16)
    rows_a, tiles_a, fock_lmo = lax.optimization_barrier((rows_a, tiles_a, fock_lmo))
    coef_b = lax.psum_scatter(
        fock_lmo,
        "col",
        scatter_dimension=0,
        tiled=True,
    )
    occ_term = jnp.einsum("ri,rj->ij", lmo_coef, coef_b, preferred_element_type=F32)
    occ_b = lax.psum(occ_term, ("row", "col")).astype(BF16)

    pres_o = lax.dynamic_index_in_dim(present, my_col, 0, keepdims=False)
    cset_o = lax.dynamic_index_in_dim(cset, my_col, 0, keepdims=False)
    pres_jk = lax.dynamic_index_in_dim(pres_o, my_row, 1, keepdims=False)
    cset_jk = lax.dynamic_index_in_dim(cset_o, my_row, 1, keepdims=False)
    rows_b = jnp.take(rows_a, cset_jk, axis=0)
    rows_b = jnp.where(pres_jk[:, None, None], rows_b, jnp.zeros_like(rows_b))
    slot_ids = jnp.broadcast_to(jnp.arange(dom_blocks, dtype=jnp.int32)[:, None], cset_o.shape)
    tiles_b = tiles_a[cset_o, slot_ids]
    tiles_b = jnp.where(pres_o[:, :, None, None], tiles_b, jnp.zeros_like(tiles_b))
    rows_dom, tiles_dom = (
        lax.all_to_all(rows_b, "row", 0, 0, tiled=True),
        lax.all_to_all(tiles_b, "row", 0, 0, tiled=True),
    )
    rows_dom = rows_dom.reshape(dom_width, -1)

    fc_a = jnp.take(coef_b.reshape(dev_blocks, BLK, occ_width), sub_o, axis=0)
    fc_a = jnp.where(has_o[:, None, None], fc_a, jnp.zeros_like(fc_a))
    fc_a = lax.all_to_all(fc_a, "col", 0, 0, tiled=True)
    fc_b = jnp.take(fc_a, cset_jk, axis=0)
    fc_b = jnp.where(pres_jk[:, None, None], fc_b, jnp.zeros_like(fc_b))
    fc_dom = lax.all_to_all(fc_b, "row", 0, 0, tiled=True).reshape(dom_width, occ_width)

    coef_dom = rows_dom[:, :occ_width]
    three_dom = rows_dom[:, occ_width:]
    correction = jnp.dot(coef_dom, occ_b, preferred_element_type=F32)
    proj_dom = (fc_dom.astype(F32) - 0.5 * correction).astype(BF16)

    slot_rot = rotation[0, 0]
    rot_tiles = slot_rot.reshape(dom_blocks, BLK, -1)
    fock_half = jnp.einsum("abtu,bun->atn", tiles_dom, rot_tiles, preferred_element_type=F32)
    fock_half = fock_half.reshape(dom_width, -1).astype(BF16)
    fock_rot = jnp.einsum("xm,xn->mn", slot_rot, fock_half, preferred_element_type=F32)
    coef_rot = jnp.einsum("xm,xi->mi", slot_rot, coef_dom, preferred_element_type=F32).astype(BF16)
    proj_rot = jnp.einsum("xm,xi->mi", slot_rot, proj_dom, preferred_element_type=F32).astype(BF16)
    proj_fock = fock_rot - jnp.einsum("mi,ni->mn", coef_rot, proj_rot, preferred_element_type=F32)
    proj_fock = proj_fock - jnp.einsum("mi,ni->mn", proj_rot, coef_rot, preferred_element_type=F32)
    three_rot = jnp.einsum("xm,xu->mu", slot_rot, three_dom, preferred_element_type=F32).astype(BF16)
    return (proj_fock[None, None], three_rot[None, None])


def solution(mesh):
    placed = (
        P("row", "col", None),
        P(("row", "col"), None),
        P(("row", "col"), None),
        P("col", "row", None, None),
        P(),
        P(),
    )
    return jax.shard_map(
        body,
        mesh=mesh,
        in_specs=placed,
        out_specs=(P("col", "row", None, None), P("col", "row", None, None)),
        check_vma=False,
    )
```

```python
import jax
import jax.numpy as jnp
from jax import lax
from jax.sharding import PartitionSpec as P

BLK = 128
F32 = jnp.float32
BF16 = jnp.bfloat16


def pick(mask, table):
    return jnp.sum(jnp.where(mask, table, 0), axis=-1)


def body(fock, lmo_coef, three_index, rotation, lmo_ids, domains):
    num_sets = lax.axis_size("col")
    my_row = lax.axis_index("row")
    my_col = lax.axis_index("col")
    dev_rows = lmo_coef.shape[0]
    occ_width = lmo_coef.shape[1]
    dev_blocks = dev_rows // BLK
    dom_blocks = domains.shape[1]
    dom_width = dom_blocks * BLK
    panel_fock = fock[:, 0, :]
    panel_blocks = panel_fock.shape[0] // BLK
    col_blocks = panel_fock.shape[1] // BLK

    doms = jnp.take(domains, lmo_ids, axis=0)
    present = doms >= 0
    clipped = jnp.maximum(doms, 0)
    flat = clipped // dev_blocks
    cset = flat % num_sets
    sub = clipped % dev_blocks
    panel = flat // num_sets
    row_tile = cset * dev_blocks + sub
    col_tile = panel * dev_blocks + sub

    pres_k = lax.dynamic_index_in_dim(present, my_row, 2, keepdims=False)
    cset_k = lax.dynamic_index_in_dim(cset, my_row, 2, keepdims=False)
    sub_k = lax.dynamic_index_in_dim(sub, my_row, 2, keepdims=False)
    rtile_k = lax.dynamic_index_in_dim(row_tile, my_row, 2, keepdims=False)
    mine_k = pres_k & (cset_k == my_col)
    has_o = jnp.any(mine_k, axis=1)
    sub_o = pick(mine_k, sub_k)
    mine2 = present & (cset == my_col)
    ct = pick(mine2, col_tile)
    ok_tile = jnp.any(mine2, axis=2) & pres_k
    fock_tiles = panel_fock.reshape(panel_blocks, BLK, col_blocks, BLK)
    tiles_a = fock_tiles[rtile_k, :, ct, :]
    tiles_a = jnp.where(ok_tile[:, :, None, None], tiles_a, jnp.zeros_like(tiles_a))
    in_rows = jnp.concatenate([lmo_coef, three_index], axis=1).reshape(dev_blocks, BLK, -1)
    rows_a = jnp.take(in_rows, sub_o, axis=0)
    rows_a = jnp.where(has_o[:, None, None], rows_a, jnp.zeros_like(rows_a))
    rows_a = lax.all_to_all(rows_a, "col", 0, 0, tiled=True)
    tiles_a, rows_a = lax.optimization_barrier((tiles_a, rows_a))
    tiles_a = lax.all_to_all(tiles_a, "col", 0, 0, tiled=True)

    gathered = lax.all_gather(lmo_coef, "row", axis=0, tiled=True)
    fock_lmo = jnp.dot(panel_fock, gathered, preferred_element_type=F32).astype(BF16)
    rows_a, tiles_a, fock_lmo = lax.optimization_barrier((rows_a, tiles_a, fock_lmo))
    coef_b = lax.psum_scatter(
        fock_lmo,
        "col",
        scatter_dimension=0,
        tiled=True,
    )
    occ_term = jnp.einsum("ri,rj->ij", lmo_coef, coef_b, preferred_element_type=F32)
    occ_b = lax.psum(occ_term, ("row", "col")).astype(BF16)

    pres_o = lax.dynamic_index_in_dim(present, my_col, 0, keepdims=False)
    cset_o = lax.dynamic_index_in_dim(cset, my_col, 0, keepdims=False)
    pres_jk = lax.dynamic_index_in_dim(pres_o, my_row, 1, keepdims=False)
    cset_jk = lax.dynamic_index_in_dim(cset_o, my_row, 1, keepdims=False)
    rows_b = jnp.take(rows_a, cset_jk, axis=0)
    rows_b = jnp.where(pres_jk[:, None, None], rows_b, jnp.zeros_like(rows_b))
    slot_ids = jnp.broadcast_to(jnp.arange(dom_blocks, dtype=jnp.int32)[:, None], cset_o.shape)
    tiles_b = tiles_a[cset_o, slot_ids]
    tiles_b = jnp.where(pres_o[:, :, None, None], tiles_b, jnp.zeros_like(tiles_b))
    rows_dom, tiles_dom = (
        lax.all_to_all(rows_b, "row", 0, 0, tiled=True),
        lax.all_to_all(tiles_b, "row", 0, 0, tiled=True),
    )
    rows_dom = rows_dom.reshape(dom_width, -1)

    fc_a = jnp.take(coef_b.reshape(dev_blocks, BLK, occ_width), sub_o, axis=0)
    fc_a = jnp.where(has_o[:, None, None], fc_a, jnp.zeros_like(fc_a))
    fc_a = lax.all_to_all(fc_a, "col", 0, 0, tiled=True)
    fc_a, occ_b, rows_dom, tiles_dom = lax.optimization_barrier((fc_a, occ_b, rows_dom, tiles_dom))
    fc_b = jnp.take(fc_a, cset_jk, axis=0)
    fc_b = jnp.where(pres_jk[:, None, None], fc_b, jnp.zeros_like(fc_b))
    fc_dom = lax.all_to_all(fc_b, "row", 0, 0, tiled=True).reshape(dom_width, occ_width)

    coef_dom = rows_dom[:, :occ_width]
    three_dom = rows_dom[:, occ_width:]
    correction = jnp.dot(coef_dom, occ_b, preferred_element_type=F32)
    proj_dom = (fc_dom.astype(F32) - 0.5 * correction).astype(BF16)

    slot_rot = rotation[0, 0]
    rot_tiles = slot_rot.reshape(dom_blocks, BLK, -1)
    fock_half = jnp.einsum("abtu,bun->atn", tiles_dom, rot_tiles, preferred_element_type=F32)
    fock_half = fock_half.reshape(dom_width, -1).astype(BF16)
    fock_rot = jnp.einsum("xm,xn->mn", slot_rot, fock_half, preferred_element_type=F32)
    coef_rot = jnp.einsum("xm,xi->mi", slot_rot, coef_dom, preferred_element_type=F32).astype(BF16)
    proj_rot = jnp.einsum("xm,xi->mi", slot_rot, proj_dom, preferred_element_type=F32).astype(BF16)
    proj_fock = fock_rot - jnp.einsum("mi,ni->mn", coef_rot, proj_rot, preferred_element_type=F32)
    proj_fock = proj_fock - jnp.einsum("mi,ni->mn", proj_rot, coef_rot, preferred_element_type=F32)
    three_rot = jnp.einsum("xm,xu->mu", slot_rot, three_dom, preferred_element_type=F32).astype(BF16)
    return (proj_fock[None, None], three_rot[None, None])


def solution(mesh):
    placed = (
        P("row", "col", None),
        P(("row", "col"), None),
        P(("row", "col"), None),
        P("col", "row", None, None),
        P(),
        P(),
    )
    return jax.shard_map(
        body,
        mesh=mesh,
        in_specs=placed,
        out_specs=(P("col", "row", None, None), P("col", "row", None, None)),
        check_vma=False,
    )
```

```python
import jax
import jax.numpy as jnp
from jax import lax
from jax.sharding import PartitionSpec as P

BLK = 128
F32 = jnp.float32
BF16 = jnp.bfloat16


def pick(mask, table):
    return jnp.sum(jnp.where(mask, table, 0), axis=-1)


def body(fock, lmo_coef, three_index, rotation, lmo_ids, domains):
    num_sets = lax.axis_size("col")
    my_row = lax.axis_index("row")
    my_col = lax.axis_index("col")
    dev_rows = lmo_coef.shape[0]
    occ_width = lmo_coef.shape[1]
    dev_blocks = dev_rows // BLK
    dom_blocks = domains.shape[1]
    dom_width = dom_blocks * BLK
    panel_fock = fock[:, 0, :]
    panel_blocks = panel_fock.shape[0] // BLK
    col_blocks = panel_fock.shape[1] // BLK

    doms = jnp.take(domains, lmo_ids, axis=0)
    present = doms >= 0
    clipped = jnp.maximum(doms, 0)
    flat = clipped // dev_blocks
    cset = flat % num_sets
    sub = clipped % dev_blocks
    panel = flat // num_sets
    row_tile = cset * dev_blocks + sub
    col_tile = panel * dev_blocks + sub

    pres_k = lax.dynamic_index_in_dim(present, my_row, 2, keepdims=False)
    cset_k = lax.dynamic_index_in_dim(cset, my_row, 2, keepdims=False)
    sub_k = lax.dynamic_index_in_dim(sub, my_row, 2, keepdims=False)
    rtile_k = lax.dynamic_index_in_dim(row_tile, my_row, 2, keepdims=False)
    mine_k = pres_k & (cset_k == my_col)
    has_o = jnp.any(mine_k, axis=1)
    sub_o = pick(mine_k, sub_k)
    mine2 = present & (cset == my_col)
    ct = pick(mine2, col_tile)
    ok_tile = jnp.any(mine2, axis=2) & pres_k
    fock_tiles = panel_fock.reshape(panel_blocks, BLK, col_blocks, BLK)
    tiles_a = fock_tiles[rtile_k, :, ct, :]
    tiles_a = jnp.where(ok_tile[:, :, None, None], tiles_a, jnp.zeros_like(tiles_a))
    in_rows = jnp.concatenate([lmo_coef, three_index], axis=1).reshape(dev_blocks, BLK, -1)
    rows_a = jnp.take(in_rows, sub_o, axis=0)
    rows_a = jnp.where(has_o[:, None, None], rows_a, jnp.zeros_like(rows_a))
    rows_a = lax.all_to_all(rows_a, "col", 0, 0, tiled=True)
    tiles_a, rows_a = lax.optimization_barrier((tiles_a, rows_a))
    tiles_a = lax.all_to_all(tiles_a, "col", 0, 0, tiled=True)

    gathered = lax.all_gather(lmo_coef, "row", axis=0, tiled=True)
    fock_lmo = jnp.dot(panel_fock, gathered, preferred_element_type=F32).astype(BF16)
    rows_a, tiles_a, fock_lmo = lax.optimization_barrier((rows_a, tiles_a, fock_lmo))
    coef_b = lax.psum_scatter(
        fock_lmo,
        "col",
        scatter_dimension=0,
        tiled=True,
    )
    occ_term = jnp.einsum("ri,rj->ij", lmo_coef, coef_b, preferred_element_type=F32)
    occ_b = lax.psum(occ_term, ("row", "col")).astype(BF16)

    pres_o = lax.dynamic_index_in_dim(present, my_col, 0, keepdims=False)
    cset_o = lax.dynamic_index_in_dim(cset, my_col, 0, keepdims=False)
    pres_jk = lax.dynamic_index_in_dim(pres_o, my_row, 1, keepdims=False)
    cset_jk = lax.dynamic_index_in_dim(cset_o, my_row, 1, keepdims=False)
    rows_b = jnp.take(rows_a, cset_jk, axis=0)
    rows_b = jnp.where(pres_jk[:, None, None], rows_b, jnp.zeros_like(rows_b))
    slot_ids = jnp.broadcast_to(jnp.arange(dom_blocks, dtype=jnp.int32)[:, None], cset_o.shape)
    tiles_b = tiles_a[cset_o, slot_ids]
    tiles_b = jnp.where(pres_o[:, :, None, None], tiles_b, jnp.zeros_like(tiles_b))
    rows_dom, tiles_dom = (
        lax.all_to_all(rows_b, "row", 0, 0, tiled=True),
        lax.all_to_all(tiles_b, "row", 0, 0, tiled=True),
    )
    rows_dom = rows_dom.reshape(dom_width, -1)

    mine_j = mine_k.T
    has_j = jnp.any(mine_j, axis=1)
    sub_j = pick(mine_j, sub_k.T)
    fc_1 = jnp.take(coef_b.reshape(dev_blocks, BLK, occ_width), sub_j, axis=0)
    fc_1 = jnp.where(has_j[:, None, None], fc_1, jnp.zeros_like(fc_1))
    fc_1 = lax.all_to_all(fc_1, "row", 0, 0, tiled=True)
    pres_j = lax.dynamic_index_in_dim(present, my_row, 1, keepdims=False)
    cset_j = lax.dynamic_index_in_dim(cset, my_row, 1, keepdims=False)
    mine_o = pres_j & (cset_j == my_col)
    has_ok = jnp.any(mine_o, axis=1)
    k_of_o = pick(mine_o, jnp.broadcast_to(jnp.arange(dom_blocks, dtype=jnp.int32), mine_o.shape))
    fc_2 = jnp.take(fc_1, k_of_o, axis=0)
    fc_2 = jnp.where(has_ok[:, None, None], fc_2, jnp.zeros_like(fc_2))
    fc_2 = lax.all_to_all(fc_2, "col", 0, 0, tiled=True)
    fc_2, occ_b, rows_dom, tiles_dom = lax.optimization_barrier((fc_2, occ_b, rows_dom, tiles_dom))
    pres_me = lax.dynamic_index_in_dim(pres_o, my_row, 0, keepdims=False)
    cset_me = lax.dynamic_index_in_dim(cset_o, my_row, 0, keepdims=False)
    fc_dom = jnp.take(fc_2, cset_me, axis=0)
    fc_dom = jnp.where(pres_me[:, None, None], fc_dom, jnp.zeros_like(fc_dom)).reshape(dom_width, occ_width)

    coef_dom = rows_dom[:, :occ_width]
    three_dom = rows_dom[:, occ_width:]
    correction = jnp.dot(coef_dom, occ_b, preferred_element_type=F32)
    proj_dom = (fc_dom.astype(F32) - 0.5 * correction).astype(BF16)

    slot_rot = rotation[0, 0]
    rot_tiles = slot_rot.reshape(dom_blocks, BLK, -1)
    fock_half = jnp.einsum("abtu,bun->atn", tiles_dom, rot_tiles, preferred_element_type=F32)
    fock_half = fock_half.reshape(dom_width, -1).astype(BF16)
    fock_rot = jnp.einsum("xm,xn->mn", slot_rot, fock_half, preferred_element_type=F32)
    coef_rot = jnp.einsum("xm,xi->mi", slot_rot, coef_dom, preferred_element_type=F32).astype(BF16)
    proj_rot = jnp.einsum("xm,xi->mi", slot_rot, proj_dom, preferred_element_type=F32).astype(BF16)
    proj_fock = fock_rot - jnp.einsum("mi,ni->mn", coef_rot, proj_rot, preferred_element_type=F32)
    proj_fock = proj_fock - jnp.einsum("mi,ni->mn", proj_rot, coef_rot, preferred_element_type=F32)
    three_rot = jnp.einsum("xm,xu->mu", slot_rot, three_dom, preferred_element_type=F32).astype(BF16)
    return (proj_fock[None, None], three_rot[None, None])


def solution(mesh):
    placed = (
        P("row", "col", None),
        P(("row", "col"), None),
        P(("row", "col"), None),
        P("col", "row", None, None),
        P(),
        P(),
    )
    return jax.shard_map(
        body,
        mesh=mesh,
        in_specs=placed,
        out_specs=(P("col", "row", None, None), P("col", "row", None, None)),
        check_vma=False,
    )
```

```python
import jax
import jax.numpy as jnp
from jax import lax
from jax.sharding import PartitionSpec as P

BLK = 128
F32 = jnp.float32
BF16 = jnp.bfloat16


def pick(mask, table):
    return jnp.sum(jnp.where(mask, table, 0), axis=-1)


def body(fock, lmo_coef, three_index, rotation, lmo_ids, domains):
    num_sets = lax.axis_size("col")
    my_row = lax.axis_index("row")
    my_col = lax.axis_index("col")
    dev_rows = lmo_coef.shape[0]
    occ_width = lmo_coef.shape[1]
    dev_blocks = dev_rows // BLK
    dom_blocks = domains.shape[1]
    dom_width = dom_blocks * BLK
    panel_fock = fock[:, 0, :]
    panel_blocks = panel_fock.shape[0] // BLK
    col_blocks = panel_fock.shape[1] // BLK

    doms = jnp.take(domains, lmo_ids, axis=0)
    present = doms >= 0
    clipped = jnp.maximum(doms, 0)
    flat = clipped // dev_blocks
    cset = flat % num_sets
    sub = clipped % dev_blocks
    panel = flat // num_sets
    row_tile = cset * dev_blocks + sub
    col_tile = panel * dev_blocks + sub

    pres_k = lax.dynamic_index_in_dim(present, my_row, 2, keepdims=False)
    cset_k = lax.dynamic_index_in_dim(cset, my_row, 2, keepdims=False)
    sub_k = lax.dynamic_index_in_dim(sub, my_row, 2, keepdims=False)
    rtile_k = lax.dynamic_index_in_dim(row_tile, my_row, 2, keepdims=False)
    mine_k = pres_k & (cset_k == my_col)
    sub_o = pick(mine_k, sub_k)
    mine2 = present & (cset == my_col)
    ct = pick(mine2, col_tile)
    fock_tiles = panel_fock.reshape(panel_blocks, BLK, col_blocks, BLK)
    tiles_a = fock_tiles[rtile_k, :, ct, :]
    in_rows = jnp.concatenate([lmo_coef, three_index], axis=1).reshape(dev_blocks, BLK, -1)
    rows_a = jnp.take(in_rows, sub_o, axis=0)
    rows_a = lax.all_to_all(rows_a, "col", 0, 0, tiled=True)
    tiles_a, rows_a = lax.optimization_barrier((tiles_a, rows_a))
    tiles_a = lax.all_to_all(tiles_a, "col", 0, 0, tiled=True)

    gathered = lax.all_gather(lmo_coef, "row", axis=0, tiled=True)
    fock_lmo = jnp.dot(panel_fock, gathered, preferred_element_type=F32).astype(BF16)
    rows_a, tiles_a, fock_lmo = lax.optimization_barrier((rows_a, tiles_a, fock_lmo))
    coef_b = lax.psum_scatter(
        fock_lmo,
        "col",
        scatter_dimension=0,
        tiled=True,
    )
    occ_term = jnp.einsum("ri,rj->ij", lmo_coef, coef_b, preferred_element_type=F32)
    occ_b = lax.psum(occ_term, ("row", "col")).astype(BF16)

    pres_o = lax.dynamic_index_in_dim(present, my_col, 0, keepdims=False)
    cset_o = lax.dynamic_index_in_dim(cset, my_col, 0, keepdims=False)
    pres_jk = lax.dynamic_index_in_dim(pres_o, my_row, 1, keepdims=False)
    cset_jk = lax.dynamic_index_in_dim(cset_o, my_row, 1, keepdims=False)
    rows_b = jnp.take(rows_a, cset_jk, axis=0)
    rows_b = jnp.where(pres_jk[:, None, None], rows_b, jnp.zeros_like(rows_b))
    slot_ids = jnp.broadcast_to(jnp.arange(dom_blocks, dtype=jnp.int32)[:, None], cset_o.shape)
    tiles_b = tiles_a[cset_o, slot_ids]
    live_b = pres_o & pres_jk[:, None]
    tiles_b = jnp.where(live_b[:, :, None, None], tiles_b, jnp.zeros_like(tiles_b))
    rows_dom, tiles_dom = (
        lax.all_to_all(rows_b, "row", 0, 0, tiled=True),
        lax.all_to_all(tiles_b, "row", 0, 0, tiled=True),
    )
    rows_dom = rows_dom.reshape(dom_width, -1)

    fc_a = jnp.take(coef_b.reshape(dev_blocks, BLK, occ_width), sub_o, axis=0)
    fc_a = lax.all_to_all(fc_a, "col", 0, 0, tiled=True)
    fc_a, occ_b, rows_dom, tiles_dom = lax.optimization_barrier((fc_a, occ_b, rows_dom, tiles_dom))
    fc_b = jnp.take(fc_a, cset_jk, axis=0)
    fc_b = jnp.where(pres_jk[:, None, None], fc_b, jnp.zeros_like(fc_b))
    fc_dom = lax.all_to_all(fc_b, "row", 0, 0, tiled=True).reshape(dom_width, occ_width)

    coef_dom = rows_dom[:, :occ_width]
    three_dom = rows_dom[:, occ_width:]
    correction = jnp.dot(coef_dom, occ_b, preferred_element_type=F32)
    proj_dom = (fc_dom.astype(F32) - 0.5 * correction).astype(BF16)

    slot_rot = rotation[0, 0]
    rot_tiles = slot_rot.reshape(dom_blocks, BLK, -1)
    fock_half = jnp.einsum("abtu,bun->atn", tiles_dom, rot_tiles, preferred_element_type=F32)
    fock_half = fock_half.reshape(dom_width, -1).astype(BF16)
    fock_rot = jnp.einsum("xm,xn->mn", slot_rot, fock_half, preferred_element_type=F32)
    coef_rot = jnp.einsum("xm,xi->mi", slot_rot, coef_dom, preferred_element_type=F32).astype(BF16)
    proj_rot = jnp.einsum("xm,xi->mi", slot_rot, proj_dom, preferred_element_type=F32).astype(BF16)
    proj_fock = fock_rot - jnp.einsum("mi,ni->mn", coef_rot, proj_rot, preferred_element_type=F32)
    proj_fock = proj_fock - jnp.einsum("mi,ni->mn", proj_rot, coef_rot, preferred_element_type=F32)
    three_rot = jnp.einsum("xm,xu->mu", slot_rot, three_dom, preferred_element_type=F32).astype(BF16)
    return (proj_fock[None, None], three_rot[None, None])


def solution(mesh):
    placed = (
        P("row", "col", None),
        P(("row", "col"), None),
        P(("row", "col"), None),
        P("col", "row", None, None),
        P(),
        P(),
    )
    return jax.shard_map(
        body,
        mesh=mesh,
        in_specs=placed,
        out_specs=(P("col", "row", None, None), P("col", "row", None, None)),
        check_vma=False,
    )
```

```python
import jax
import jax.numpy as jnp
from jax import lax
from jax.sharding import PartitionSpec as P

BLK = 128
F32 = jnp.float32
BF16 = jnp.bfloat16


def pick(mask, table):
    return jnp.sum(jnp.where(mask, table, 0), axis=-1)


def body(fock, lmo_coef, three_index, rotation, lmo_ids, domains):
    num_sets = lax.axis_size("col")
    my_row = lax.axis_index("row")
    my_col = lax.axis_index("col")
    dev_rows = lmo_coef.shape[0]
    occ_width = lmo_coef.shape[1]
    dev_blocks = dev_rows // BLK
    dom_blocks = domains.shape[1]
    dom_width = dom_blocks * BLK
    panel_fock = fock[:, 0, :]
    panel_blocks = panel_fock.shape[0] // BLK
    col_blocks = panel_fock.shape[1] // BLK

    doms = jnp.take(domains, lmo_ids, axis=0)
    present = doms >= 0
    clipped = jnp.maximum(doms, 0)
    flat = clipped // dev_blocks
    cset = flat % num_sets
    sub = clipped % dev_blocks
    panel = flat // num_sets
    row_tile = cset * dev_blocks + sub
    col_tile = panel * dev_blocks + sub

    pres_k = lax.dynamic_index_in_dim(present, my_row, 2, keepdims=False)
    cset_k = lax.dynamic_index_in_dim(cset, my_row, 2, keepdims=False)
    sub_k = lax.dynamic_index_in_dim(sub, my_row, 2, keepdims=False)
    rtile_k = lax.dynamic_index_in_dim(row_tile, my_row, 2, keepdims=False)
    mine_k = pres_k & (cset_k == my_col)
    sub_o = pick(mine_k, sub_k)
    mine2 = present & (cset == my_col)
    ct = pick(mine2, col_tile)
    fock_tiles = panel_fock.reshape(panel_blocks, BLK, col_blocks, BLK)
    tiles_a = fock_tiles[rtile_k, :, ct, :]
    in_rows = jnp.concatenate([lmo_coef, three_index], axis=1).reshape(dev_blocks, BLK, -1)
    rows_a = jnp.take(in_rows, sub_o, axis=0)
    rows_a = lax.all_to_all(rows_a, "col", 0, 0, tiled=True)
    tiles_a, rows_a = lax.optimization_barrier((tiles_a, rows_a))
    tiles_a = lax.all_to_all(tiles_a, "col", 0, 0, tiled=True)

    gathered = lax.all_gather(lmo_coef, "row", axis=0, tiled=True)
    fock_lmo = jnp.dot(panel_fock, gathered, preferred_element_type=F32).astype(BF16)
    rows_a, tiles_a, fock_lmo = lax.optimization_barrier((rows_a, tiles_a, fock_lmo))
    half = occ_width // 2
    coef_lo = lax.psum_scatter(fock_lmo[:, :half], "col", scatter_dimension=0, tiled=True)
    coef_hi = lax.psum_scatter(fock_lmo[:, half:], "col", scatter_dimension=0, tiled=True)
    occ_lo = jnp.einsum("ri,rj->ij", lmo_coef, coef_lo, preferred_element_type=F32)
    occ_lo = lax.psum(occ_lo, ("row", "col")).astype(BF16)
    coef_hi, occ_lo = lax.optimization_barrier((coef_hi, occ_lo))
    occ_hi = jnp.einsum("ri,rj->ij", lmo_coef, coef_hi, preferred_element_type=F32)
    occ_hi = lax.psum(occ_hi, ("row", "col")).astype(BF16)
    coef_b = jnp.concatenate([coef_lo, coef_hi], axis=1)
    occ_b = jnp.concatenate([occ_lo, occ_hi], axis=1)

    pres_o = lax.dynamic_index_in_dim(present, my_col, 0, keepdims=False)
    cset_o = lax.dynamic_index_in_dim(cset, my_col, 0, keepdims=False)
    pres_jk = lax.dynamic_index_in_dim(pres_o, my_row, 1, keepdims=False)
    cset_jk = lax.dynamic_index_in_dim(cset_o, my_row, 1, keepdims=False)
    rows_b = jnp.take(rows_a, cset_jk, axis=0)
    rows_b = jnp.where(pres_jk[:, None, None], rows_b, jnp.zeros_like(rows_b))
    slot_ids = jnp.broadcast_to(jnp.arange(dom_blocks, dtype=jnp.int32)[:, None], cset_o.shape)
    tiles_b = tiles_a[cset_o, slot_ids]
    live_b = pres_o & pres_jk[:, None]
    tiles_b = jnp.where(live_b[:, :, None, None], tiles_b, jnp.zeros_like(tiles_b))
    rows_dom, tiles_dom = (
        lax.all_to_all(rows_b, "row", 0, 0, tiled=True),
        lax.all_to_all(tiles_b, "row", 0, 0, tiled=True),
    )
    rows_dom = rows_dom.reshape(dom_width, -1)

    fc_a = jnp.take(coef_b.reshape(dev_blocks, BLK, occ_width), sub_o, axis=0)
    fc_a = lax.all_to_all(fc_a, "col", 0, 0, tiled=True)
    fc_a, occ_b, rows_dom, tiles_dom = lax.optimization_barrier((fc_a, occ_b, rows_dom, tiles_dom))
    fc_b = jnp.take(fc_a, cset_jk, axis=0)
    fc_b = jnp.where(pres_jk[:, None, None], fc_b, jnp.zeros_like(fc_b))
    fc_dom = lax.all_to_all(fc_b, "row", 0, 0, tiled=True).reshape(dom_width, occ_width)

    coef_dom = rows_dom[:, :occ_width]
    three_dom = rows_dom[:, occ_width:]
    correction = jnp.dot(coef_dom, occ_b, preferred_element_type=F32)
    proj_dom = (fc_dom.astype(F32) - 0.5 * correction).astype(BF16)

    slot_rot = rotation[0, 0]
    rot_tiles = slot_rot.reshape(dom_blocks, BLK, -1)
    fock_half = jnp.einsum("abtu,bun->atn", tiles_dom, rot_tiles, preferred_element_type=F32)
    fock_half = fock_half.reshape(dom_width, -1).astype(BF16)
    fock_rot = jnp.einsum("xm,xn->mn", slot_rot, fock_half, preferred_element_type=F32)
    coef_rot = jnp.einsum("xm,xi->mi", slot_rot, coef_dom, preferred_element_type=F32).astype(BF16)
    proj_rot = jnp.einsum("xm,xi->mi", slot_rot, proj_dom, preferred_element_type=F32).astype(BF16)
    proj_fock = fock_rot - jnp.einsum("mi,ni->mn", coef_rot, proj_rot, preferred_element_type=F32)
    proj_fock = proj_fock - jnp.einsum("mi,ni->mn", proj_rot, coef_rot, preferred_element_type=F32)
    three_rot = jnp.einsum("xm,xu->mu", slot_rot, three_dom, preferred_element_type=F32).astype(BF16)
    return (proj_fock[None, None], three_rot[None, None])


def solution(mesh):
    placed = (
        P("row", "col", None),
        P(("row", "col"), None),
        P(("row", "col"), None),
        P("col", "row", None, None),
        P(),
        P(),
    )
    return jax.shard_map(
        body,
        mesh=mesh,
        in_specs=placed,
        out_specs=(P("col", "row", None, None), P("col", "row", None, None)),
        check_vma=False,
    )
```

```python
import jax
import jax.numpy as jnp
from jax import lax
from jax.sharding import PartitionSpec as P

BLK = 128
F32 = jnp.float32
BF16 = jnp.bfloat16


def pick(mask, table):
    return jnp.sum(jnp.where(mask, table, 0), axis=-1)


def body(fock, lmo_coef, three_index, rotation, lmo_ids, domains):
    num_sets = lax.axis_size("col")
    my_row = lax.axis_index("row")
    my_col = lax.axis_index("col")
    dev_rows = lmo_coef.shape[0]
    occ_width = lmo_coef.shape[1]
    dev_blocks = dev_rows // BLK
    dom_blocks = domains.shape[1]
    dom_width = dom_blocks * BLK
    panel_fock = fock[:, 0, :]
    panel_blocks = panel_fock.shape[0] // BLK
    col_blocks = panel_fock.shape[1] // BLK

    doms = jnp.take(domains, lmo_ids, axis=0)
    present = doms >= 0
    clipped = jnp.maximum(doms, 0)
    flat = clipped // dev_blocks
    cset = flat % num_sets
    sub = clipped % dev_blocks
    panel = flat // num_sets
    row_tile = cset * dev_blocks + sub
    col_tile = panel * dev_blocks + sub

    pres_k = lax.dynamic_index_in_dim(present, my_row, 2, keepdims=False)
    cset_k = lax.dynamic_index_in_dim(cset, my_row, 2, keepdims=False)
    sub_k = lax.dynamic_index_in_dim(sub, my_row, 2, keepdims=False)
    rtile_k = lax.dynamic_index_in_dim(row_tile, my_row, 2, keepdims=False)
    mine_k = pres_k & (cset_k == my_col)
    sub_o = pick(mine_k, sub_k)
    mine2 = present & (cset == my_col)
    ct = pick(mine2, col_tile)
    fock_tiles = panel_fock.reshape(panel_blocks, BLK, col_blocks, BLK)
    tiles_a = fock_tiles[rtile_k, :, ct, :]
    in_rows = jnp.concatenate([lmo_coef, three_index], axis=1).reshape(dev_blocks, BLK, -1)
    rows_a = jnp.take(in_rows, sub_o, axis=0)
    rows_a = lax.all_to_all(rows_a, "col", 0, 0, tiled=True)
    tiles_a, rows_a = lax.optimization_barrier((tiles_a, rows_a))
    tiles_a = lax.all_to_all(tiles_a, "col", 0, 0, tiled=True)

    gathered = lax.all_gather(lmo_coef, "row", axis=0, tiled=True)
    fock_lmo = jnp.dot(panel_fock, gathered, preferred_element_type=F32).astype(BF16)
    rows_a, fock_lmo = lax.optimization_barrier((rows_a, fock_lmo))
    coef_b = lax.psum_scatter(
        fock_lmo,
        "col",
        scatter_dimension=0,
        tiled=True,
    )
    occ_term = jnp.einsum("ri,rj->ij", lmo_coef, coef_b, preferred_element_type=F32)
    occ_b = lax.psum(occ_term, ("row", "col")).astype(BF16)

    pres_o = lax.dynamic_index_in_dim(present, my_col, 0, keepdims=False)
    cset_o = lax.dynamic_index_in_dim(cset, my_col, 0, keepdims=False)
    pres_jk = lax.dynamic_index_in_dim(pres_o, my_row, 1, keepdims=False)
    cset_jk = lax.dynamic_index_in_dim(cset_o, my_row, 1, keepdims=False)
    rows_b = jnp.take(rows_a, cset_jk, axis=0)
    rows_b = jnp.where(pres_jk[:, None, None], rows_b, jnp.zeros_like(rows_b))
    slot_ids = jnp.broadcast_to(jnp.arange(dom_blocks, dtype=jnp.int32)[:, None], cset_o.shape)
    tiles_b = tiles_a[cset_o, slot_ids]
    live_b = pres_o & pres_jk[:, None]
    tiles_b = jnp.where(live_b[:, :, None, None], tiles_b, jnp.zeros_like(tiles_b))
    rows_dom, tiles_dom = (
        lax.all_to_all(rows_b, "row", 0, 0, tiled=True),
        lax.all_to_all(tiles_b, "row", 0, 0, tiled=True),
    )
    rows_dom = rows_dom.reshape(dom_width, -1)

    fc_a = jnp.take(coef_b.reshape(dev_blocks, BLK, occ_width), sub_o, axis=0)
    fc_a = lax.all_to_all(fc_a, "col", 0, 0, tiled=True)
    fc_a, occ_b, rows_dom, tiles_dom = lax.optimization_barrier((fc_a, occ_b, rows_dom, tiles_dom))
    fc_b = jnp.take(fc_a, cset_jk, axis=0)
    fc_b = jnp.where(pres_jk[:, None, None], fc_b, jnp.zeros_like(fc_b))
    fc_dom = lax.all_to_all(fc_b, "row", 0, 0, tiled=True).reshape(dom_width, occ_width)

    coef_dom = rows_dom[:, :occ_width]
    three_dom = rows_dom[:, occ_width:]
    correction = jnp.dot(coef_dom, occ_b, preferred_element_type=F32)
    proj_dom = (fc_dom.astype(F32) - 0.5 * correction).astype(BF16)

    slot_rot = rotation[0, 0]
    rot_tiles = slot_rot.reshape(dom_blocks, BLK, -1)
    fock_half = jnp.einsum("abtu,bun->atn", tiles_dom, rot_tiles, preferred_element_type=F32)
    fock_half = fock_half.reshape(dom_width, -1).astype(BF16)
    fock_rot = jnp.einsum("xm,xn->mn", slot_rot, fock_half, preferred_element_type=F32)
    coef_rot = jnp.einsum("xm,xi->mi", slot_rot, coef_dom, preferred_element_type=F32).astype(BF16)
    proj_rot = jnp.einsum("xm,xi->mi", slot_rot, proj_dom, preferred_element_type=F32).astype(BF16)
    proj_fock = fock_rot - jnp.einsum("mi,ni->mn", coef_rot, proj_rot, preferred_element_type=F32)
    proj_fock = proj_fock - jnp.einsum("mi,ni->mn", proj_rot, coef_rot, preferred_element_type=F32)
    three_rot = jnp.einsum("xm,xu->mu", slot_rot, three_dom, preferred_element_type=F32).astype(BF16)
    return (proj_fock[None, None], three_rot[None, None])


def solution(mesh):
    placed = (
        P("row", "col", None),
        P(("row", "col"), None),
        P(("row", "col"), None),
        P("col", "row", None, None),
        P(),
        P(),
    )
    return jax.shard_map(
        body,
        mesh=mesh,
        in_specs=placed,
        out_specs=(P("col", "row", None, None), P("col", "row", None, None)),
        check_vma=False,
    )
```

```python
import jax
import jax.numpy as jnp
from jax import lax
from jax.sharding import PartitionSpec as P

BLK = 128
F32 = jnp.float32
BF16 = jnp.bfloat16


def pick(mask, table):
    return jnp.sum(jnp.where(mask, table, 0), axis=-1)


def body(fock, lmo_coef, three_index, rotation, lmo_ids, domains):
    num_sets = lax.axis_size("col")
    my_row = lax.axis_index("row")
    my_col = lax.axis_index("col")
    dev_rows = lmo_coef.shape[0]
    occ_width = lmo_coef.shape[1]
    dev_blocks = dev_rows // BLK
    dom_blocks = domains.shape[1]
    dom_width = dom_blocks * BLK
    panel_fock = fock[:, 0, :]
    panel_blocks = panel_fock.shape[0] // BLK
    col_blocks = panel_fock.shape[1] // BLK

    doms = jnp.take(domains, lmo_ids, axis=0)
    present = doms >= 0
    clipped = jnp.maximum(doms, 0)
    flat = clipped // dev_blocks
    cset = flat % num_sets
    sub = clipped % dev_blocks
    panel = flat // num_sets
    row_tile = cset * dev_blocks + sub
    col_tile = panel * dev_blocks + sub

    pres_k = lax.dynamic_index_in_dim(present, my_row, 2, keepdims=False)
    cset_k = lax.dynamic_index_in_dim(cset, my_row, 2, keepdims=False)
    sub_k = lax.dynamic_index_in_dim(sub, my_row, 2, keepdims=False)
    rtile_k = lax.dynamic_index_in_dim(row_tile, my_row, 2, keepdims=False)
    mine_k = pres_k & (cset_k == my_col)
    sub_o = pick(mine_k, sub_k)
    mine2 = present & (cset == my_col)
    ct = pick(mine2, col_tile)
    fock_tiles = panel_fock.reshape(panel_blocks, BLK, col_blocks, BLK)
    tiles_a = fock_tiles.at[rtile_k, :, ct, :].get(mode="promise_in_bounds")
    in_rows = jnp.concatenate([lmo_coef, three_index], axis=1).reshape(dev_blocks, BLK, -1)
    rows_a = jnp.take(in_rows, sub_o, axis=0, mode="clip")
    rows_a = lax.all_to_all(rows_a, "col", 0, 0, tiled=True)
    tiles_a, rows_a = lax.optimization_barrier((tiles_a, rows_a))
    tiles_a = lax.all_to_all(tiles_a, "col", 0, 0, tiled=True)

    gathered = lax.all_gather(lmo_coef, "row", axis=0, tiled=True)
    fock_lmo = jnp.dot(panel_fock, gathered, preferred_element_type=F32).astype(BF16)
    rows_a, tiles_a, fock_lmo = lax.optimization_barrier((rows_a, tiles_a, fock_lmo))
    coef_b = lax.psum_scatter(
        fock_lmo,
        "col",
        scatter_dimension=0,
        tiled=True,
    )
    occ_term = jnp.einsum("ri,rj->ij", lmo_coef, coef_b, preferred_element_type=F32)
    occ_b = lax.psum(occ_term, ("row", "col")).astype(BF16)

    pres_o = lax.dynamic_index_in_dim(present, my_col, 0, keepdims=False)
    cset_o = lax.dynamic_index_in_dim(cset, my_col, 0, keepdims=False)
    pres_jk = lax.dynamic_index_in_dim(pres_o, my_row, 1, keepdims=False)
    cset_jk = lax.dynamic_index_in_dim(cset_o, my_row, 1, keepdims=False)
    rows_b = jnp.take(rows_a, cset_jk, axis=0, mode="clip")
    rows_b = jnp.where(pres_jk[:, None, None], rows_b, jnp.zeros_like(rows_b))
    slot_ids = jnp.broadcast_to(jnp.arange(dom_blocks, dtype=jnp.int32)[:, None], cset_o.shape)
    tiles_b = tiles_a.at[cset_o, slot_ids].get(mode="promise_in_bounds")
    live_b = pres_o & pres_jk[:, None]
    tiles_b = jnp.where(live_b[:, :, None, None], tiles_b, jnp.zeros_like(tiles_b))
    rows_dom, tiles_dom = (
        lax.all_to_all(rows_b, "row", 0, 0, tiled=True),
        lax.all_to_all(tiles_b, "row", 0, 0, tiled=True),
    )
    rows_dom = rows_dom.reshape(dom_width, -1)

    fc_a = jnp.take(coef_b.reshape(dev_blocks, BLK, occ_width), sub_o, axis=0, mode="clip")
    fc_a = lax.all_to_all(fc_a, "col", 0, 0, tiled=True)
    fc_a, occ_b, rows_dom, tiles_dom = lax.optimization_barrier((fc_a, occ_b, rows_dom, tiles_dom))
    fc_b = jnp.take(fc_a, cset_jk, axis=0, mode="clip")
    fc_b = jnp.where(pres_jk[:, None, None], fc_b, jnp.zeros_like(fc_b))
    fc_dom = lax.all_to_all(fc_b, "row", 0, 0, tiled=True).reshape(dom_width, occ_width)

    coef_dom = rows_dom[:, :occ_width]
    three_dom = rows_dom[:, occ_width:]
    correction = jnp.dot(coef_dom, occ_b, preferred_element_type=F32)
    proj_dom = (fc_dom.astype(F32) - 0.5 * correction).astype(BF16)

    slot_rot = rotation[0, 0]
    rot_tiles = slot_rot.reshape(dom_blocks, BLK, -1)
    fock_half = jnp.einsum("abtu,bun->atn", tiles_dom, rot_tiles, preferred_element_type=F32)
    fock_half = fock_half.reshape(dom_width, -1).astype(BF16)
    fock_rot = jnp.einsum("xm,xn->mn", slot_rot, fock_half, preferred_element_type=F32)
    coef_rot = jnp.einsum("xm,xi->mi", slot_rot, coef_dom, preferred_element_type=F32).astype(BF16)
    proj_rot = jnp.einsum("xm,xi->mi", slot_rot, proj_dom, preferred_element_type=F32).astype(BF16)
    proj_fock = fock_rot - jnp.einsum("mi,ni->mn", coef_rot, proj_rot, preferred_element_type=F32)
    proj_fock = proj_fock - jnp.einsum("mi,ni->mn", proj_rot, coef_rot, preferred_element_type=F32)
    three_rot = jnp.einsum("xm,xu->mu", slot_rot, three_dom, preferred_element_type=F32).astype(BF16)
    return (proj_fock[None, None], three_rot[None, None])


def solution(mesh):
    placed = (
        P("row", "col", None),
        P(("row", "col"), None),
        P(("row", "col"), None),
        P("col", "row", None, None),
        P(),
        P(),
    )
    return jax.shard_map(
        body,
        mesh=mesh,
        in_specs=placed,
        out_specs=(P("col", "row", None, None), P("col", "row", None, None)),
        check_vma=False,
    )
```

```python
import jax
import jax.numpy as jnp
from jax import lax
from jax.sharding import PartitionSpec as P

BLK = 128
F32 = jnp.float32
BF16 = jnp.bfloat16


def pick(mask, table):
    return jnp.sum(jnp.where(mask, table, 0), axis=-1)


def body(fock, lmo_coef, three_index, rotation, lmo_ids, domains):
    num_sets = lax.axis_size("col")
    my_row = lax.axis_index("row")
    my_col = lax.axis_index("col")
    dev_rows = lmo_coef.shape[0]
    occ_width = lmo_coef.shape[1]
    dev_blocks = dev_rows // BLK
    dom_blocks = domains.shape[1]
    dom_width = dom_blocks * BLK
    panel_fock = fock[:, 0, :]
    panel_blocks = panel_fock.shape[0] // BLK
    col_blocks = panel_fock.shape[1] // BLK

    doms = jnp.take(domains, lmo_ids, axis=0, mode="clip")
    present = doms >= 0
    clipped = jnp.maximum(doms, 0)
    flat = clipped // dev_blocks
    cset = flat % num_sets
    sub = clipped % dev_blocks
    panel = flat // num_sets
    row_tile = cset * dev_blocks + sub
    col_tile = panel * dev_blocks + sub

    pres_k = lax.dynamic_index_in_dim(present, my_row, 2, keepdims=False)
    cset_k = lax.dynamic_index_in_dim(cset, my_row, 2, keepdims=False)
    sub_k = lax.dynamic_index_in_dim(sub, my_row, 2, keepdims=False)
    rtile_k = lax.dynamic_index_in_dim(row_tile, my_row, 2, keepdims=False)
    mine_k = pres_k & (cset_k == my_col)
    sub_o = pick(mine_k, sub_k)
    mine2 = present & (cset == my_col)
    ct = pick(mine2, col_tile)
    fock_tiles = panel_fock.reshape(panel_blocks, BLK, col_blocks, BLK)
    tiles_a = fock_tiles.at[rtile_k, :, ct, :].get(mode="promise_in_bounds")
    in_rows = jnp.concatenate([lmo_coef, three_index], axis=1).reshape(dev_blocks, BLK, -1)
    rows_a = jnp.take(in_rows, sub_o, axis=0, mode="clip")
    rows_a = lax.all_to_all(rows_a, "col", 0, 0, tiled=True)
    tiles_a, rows_a = lax.optimization_barrier((tiles_a, rows_a))
    tiles_a = lax.all_to_all(tiles_a, "col", 0, 0, tiled=True)

    gathered = lax.all_gather(lmo_coef, "row", axis=0, tiled=True)
    fock_lmo = jnp.dot(panel_fock, gathered, preferred_element_type=F32).astype(BF16)
    rows_a, tiles_a, fock_lmo = lax.optimization_barrier((rows_a, tiles_a, fock_lmo))
    coef_b = lax.psum_scatter(
        fock_lmo,
        "col",
        scatter_dimension=0,
        tiled=True,
    )
    occ_term = jnp.einsum("ri,rj->ij", lmo_coef, coef_b, preferred_element_type=F32)
    occ_b = lax.psum(occ_term, ("row", "col")).astype(BF16)

    pres_o = lax.dynamic_index_in_dim(present, my_col, 0, keepdims=False)
    cset_o = lax.dynamic_index_in_dim(cset, my_col, 0, keepdims=False)
    pres_jk = lax.dynamic_index_in_dim(pres_o, my_row, 1, keepdims=False)
    cset_jk = lax.dynamic_index_in_dim(cset_o, my_row, 1, keepdims=False)
    rows_b = jnp.take(rows_a, cset_jk, axis=0, mode="clip")
    rows_b = jnp.where(pres_jk[:, None, None], rows_b, jnp.zeros_like(rows_b))
    slot_ids = jnp.broadcast_to(jnp.arange(dom_blocks, dtype=jnp.int32)[:, None], cset_o.shape)
    tiles_b = tiles_a.at[cset_o, slot_ids].get(mode="promise_in_bounds")
    live_b = pres_o & pres_jk[:, None]
    tiles_b = jnp.where(live_b[:, :, None, None], tiles_b, jnp.zeros_like(tiles_b))
    rows_dom, tiles_dom = (
        lax.all_to_all(rows_b, "row", 0, 0, tiled=True),
        lax.all_to_all(tiles_b, "row", 0, 0, tiled=True),
    )
    rows_dom = rows_dom.reshape(dom_width, -1)

    fc_a = jnp.take(coef_b.reshape(dev_blocks, BLK, occ_width), sub_o, axis=0, mode="clip")
    fc_a = lax.all_to_all(fc_a, "col", 0, 0, tiled=True)
    fc_a, occ_b, rows_dom, tiles_dom = lax.optimization_barrier((fc_a, occ_b, rows_dom, tiles_dom))
    fc_b = jnp.take(fc_a, cset_jk, axis=0, mode="clip")
    fc_dom = lax.all_to_all(fc_b, "row", 0, 0, tiled=True).reshape(dom_width, occ_width)
    pres_me = lax.dynamic_index_in_dim(pres_o, my_row, 0, keepdims=False)
    row_live = jnp.repeat(pres_me, BLK, total_repeat_length=dom_width)

    coef_dom = rows_dom[:, :occ_width]
    three_dom = rows_dom[:, occ_width:]
    correction = jnp.dot(coef_dom, occ_b, preferred_element_type=F32)
    fc_dom = jnp.where(row_live[:, None], fc_dom, jnp.zeros_like(fc_dom))
    proj_dom = (fc_dom.astype(F32) - 0.5 * correction).astype(BF16)

    slot_rot = rotation[0, 0]
    rot_tiles = slot_rot.reshape(dom_blocks, BLK, -1)
    fock_half = jnp.einsum("abtu,bun->atn", tiles_dom, rot_tiles, preferred_element_type=F32)
    fock_half = fock_half.reshape(dom_width, -1).astype(BF16)
    fock_rot = jnp.einsum("xm,xn->mn", slot_rot, fock_half, preferred_element_type=F32)
    coef_rot = jnp.einsum("xm,xi->mi", slot_rot, coef_dom, preferred_element_type=F32).astype(BF16)
    proj_rot = jnp.einsum("xm,xi->mi", slot_rot, proj_dom, preferred_element_type=F32).astype(BF16)
    proj_fock = fock_rot - jnp.einsum("mi,ni->mn", coef_rot, proj_rot, preferred_element_type=F32)
    proj_fock = proj_fock - jnp.einsum("mi,ni->mn", proj_rot, coef_rot, preferred_element_type=F32)
    three_rot = jnp.einsum("xm,xu->mu", slot_rot, three_dom, preferred_element_type=F32).astype(BF16)
    return (proj_fock[None, None], three_rot[None, None])


def solution(mesh):
    placed = (
        P("row", "col", None),
        P(("row", "col"), None),
        P(("row", "col"), None),
        P("col", "row", None, None),
        P(),
        P(),
    )
    return jax.shard_map(
        body,
        mesh=mesh,
        in_specs=placed,
        out_specs=(P("col", "row", None, None), P("col", "row", None, None)),
        check_vma=False,
    )
```
